256 devices in a mesh: head: 2 (over core), blk: 128 (over x, z, y).
Axes of the slice: x: 4, y: 4, z: 8, core: 2. Of those that a mesh axis runs over, the one named last changes fastest.
Arguments:
- queries: bfloat16 [32768, 1024], P('blk', 'head'), may hold values from -5.5 to 5.5
- new_keys: bfloat16 [32768, 1024], P('blk', 'head'), may hold values from -5.5 to 5.5
- new_values: bfloat16 [32768, 1024], P('blk', 'head'), may hold values from -6 to 6
- sink_keys: bfloat16 [128, 4, 1024], P('blk', None, 'head'), may hold values from -16 to 16
- sink_values: bfloat16 [128, 4, 1024], P('blk', None, 'head'), may hold values from -6 to 6
- pool_keys: bfloat16 [128, 9, 512, 1024], P('blk', None, None, 'head'), may hold values from -6 to 6
- pool_values: bfloat16 [128, 9, 512, 1024], P('blk', None, None, 'head'), may hold values from -6 to 6
- block_ids: int32 [128, 9], replicated, may hold values from 1 to 64, as said below
- cache_lengths: int32 [128], replicated, may hold values from 4608 to 32768, as said below
- cross_keys: bfloat16 [128, 128, 1024], P('blk', None, 'head'), may hold values from -6 to 6
- cross_values: bfloat16 [128, 128, 1024], P('blk', None, 'head'), may hold values from -6 to 6
- enc_lengths: int32 [128], P('blk'), may hold values from 32 to 128
- hidden: bfloat16 [32768, 1024], P('blk', 'head'), may hold values from -6 to 6
- w_out_t: bfloat16 [1024, 1024], P(None, 'head'), may hold values from -0.1875 to 0.1875
- gain_self: float32 [1024], replicated, may hold values from 0.25 to 1.75
- bias_self: float32 [1024], replicated, may hold values from -0.5 to 0.5
- w_cross_q: bfloat16 [1024, 1024], P(None, 'head'), may hold values from -0.1875 to 0.1875
- w_cross_out_t: bfloat16 [1024, 1024], P(None, 'head'), may hold values from -0.1875 to 0.1875
- gain_cross: float32 [1024], replicated, may hold values from 0.25 to 1.75
- bias_cross: float32 [1024], replicated, may hold values from -0.5 to 0.5
Outputs:
- layer_out: bfloat16 [32768, 1024], P('blk', 'head')
The draws below stay inside these ranges and needn't reach their ends.
Inputs may be any that keep to these rules, and one draw needn't show every extreme that they name: `cache_lengths`: one request has exactly 32768 cached tokens and another exactly 4608. `block_ids`: entry [g, s] belongs to request (g - s - 1) mod 128; the 9 entries of request r hold the consecutive block numbers from (cache_lengths[r] - 4095) // 512 on, each once, in an order drawn from the seed.
All inputs are finite; a program needn't handle non-finite values.
Results may differ from the reference program's by a relative error of at most 0.02.
Values may be sent and summed in bfloat16 or wider, within the bound.
No kernel may reach another device: no remote copies, remote signals or barrier semaphores. Data moves between devices by JAX's collectives and lax.ppermute only.
A program may use at most 192 MiB of HBM per device.

```python
import jax
import jax.numpy as jnp
from jax import lax

D = 1024
H = 16
HD = 64
BS = 512
WINDOW = 4096
SINK = 4
MAXLEN = 32768
SPAN = 256
ENC = 128
HH = 1024
SLOTS = 9
REQS = 128
TOKENS = 32768


def length_table(key):
    base_key = jax.random.fold_in(key, 101)
    first_key = jax.random.fold_in(base_key, 1)
    second_key = jax.random.fold_in(base_key, 2)
    third_key = jax.random.fold_in(base_key, 3)
    lowest = WINDOW + BS
    highest = MAXLEN
    drawn = jax.random.randint(first_key, (REQS,), lowest, highest + 1)
    top_slot = jax.random.randint(second_key, (), 0, REQS)
    low_slot = (top_slot + 1 + jax.random.randint(third_key, (), 0, REQS - 1)) % REQS
    index_row = jnp.arange(REQS)
    drawn = jnp.where(index_row == top_slot, highest, drawn)
    drawn = jnp.where(index_row == low_slot, lowest, drawn)
    return drawn.astype(jnp.int32)


def draw_cache_lengths(key, part):
    return length_table(key)


def draw_block_ids(key, part):
    lengths_all = length_table(key)
    order_keys = jax.random.split(jax.random.fold_in(key, 202), REQS)
    orders = jax.vmap(lambda one_key: jax.random.permutation(one_key, SLOTS))(order_keys)
    first_block = (lengths_all - WINDOW + 1) // BS
    holder_row = jnp.arange(REQS)[:, None]
    slot_col = jnp.arange(SLOTS)[None, :]
    request_of = (holder_row - slot_col - 1) % REQS
    return (first_block[request_of] + orders[request_of, slot_col]).astype(jnp.int32)


def drawn_pair(key):
    query_key = jax.random.fold_in(key, 11)
    other_key = jax.random.fold_in(key, 12)
    query_base = jnp.clip(jax.random.normal(query_key, (TOKENS, HH), jnp.float32), -5.5, 5.5)
    key_base = jnp.clip(jax.random.normal(other_key, (TOKENS, HH), jnp.float32), -5.5, 5.5)
    return (query_base, key_base)


def draw_queries(key, part):
    return drawn_pair(key)[0].astype(jnp.bfloat16)


def draw_new_keys(key, part):
    return drawn_pair(key)[1].astype(jnp.bfloat16)


def place_ends(values, own_key, smallest, high):
    spot = [jax.random.randint(jax.random.fold_in(own_key, axis), (), 0, length) for axis, length in enumerate(values.shape)]
    longest = values.shape.index(max(values.shape))
    neighbour = spot[:longest] + [(spot[longest] + 1) % values.shape[longest]] + spot[longest + 1:]
    return values.at[tuple(spot)].set(smallest).at[tuple(neighbour)].set(high)


def block_levels(stream_key, extent, cuts, least, largest):
    level, own = 1.0, jax.random.fold_in(stream_key, 6)
    for position, parts in cuts:
        steps = jnp.exp(jax.random.uniform(jax.random.fold_in(own, position), (parts,), jnp.float32, least / len(cuts), largest / len(cuts)))
        level = level * jnp.repeat(steps, extent[position] // parts).reshape([-1 if axis == position else 1 for axis in range(len(extent))])
    return level


def centred(key, shape, scale, limit, cuts=(), kind=jnp.bfloat16):
    values = scale * jax.random.normal(key, shape, jnp.float32)
    if cuts:
        values = values * block_levels(key, shape, cuts, -0.22, 0.18)
    return jnp.clip(values, -limit, limit).astype(kind)


def setup_inputs(seed: int = 0) -> dict:
    key_list = jax.random.split(jax.random.key(seed), 21)
    queries = draw_queries(jax.random.fold_in(key_list[20], 71), 0)
    new_keys = draw_new_keys(jax.random.fold_in(key_list[20], 71), 0)
    new_values = centred(key_list[2], (TOKENS, HH), 1.0, 6.0, ((0, 128), (1, 2)))
    sink_keys = centred(key_list[3], (REQS, SINK, HH), 3.0, 16.0, ((0, 128), (2, 2)))
    sink_values = centred(key_list[4], (REQS, SINK, HH), 1.0, 6.0, ((0, 128), (2, 2)))
    pool_keys = centred(key_list[5], (REQS, SLOTS, BS, HH), 1.0, 6.0, ((0, 128), (3, 2)))
    pool_values = centred(key_list[6], (REQS, SLOTS, BS, HH), 1.0, 6.0, ((0, 128), (3, 2)))
    block_ids = draw_block_ids(jax.random.fold_in(key_list[20], 71), 0)
    cache_lengths = draw_cache_lengths(jax.random.fold_in(key_list[20], 71), 0)
    cross_keys = centred(key_list[9], (REQS, ENC, HH), 1.0, 6.0, ((0, 128), (2, 2)))
    cross_values = centred(key_list[10], (REQS, ENC, HH), 1.0, 6.0, ((0, 128), (2, 2)))
    enc_lengths = place_ends(jax.random.randint(key_list[11], (REQS,), ENC // 4, ENC + 1), jax.random.fold_in(key_list[11], 1), ENC // 4, ENC).astype(jnp.int32)
    hidden = centred(key_list[12], (TOKENS, D), 1.0, 6.0, ((0, 128), (1, 2)))
    w_out_t = centred(key_list[13], (D, HH), HH ** -0.5, 0.1875, ((1, 2),))
    gain_self = jnp.clip(1.0 + 0.15 * jax.random.normal(key_list[14], (D,), jnp.float32), 0.25, 1.75)
    bias_self = jnp.clip(jax.random.uniform(key_list[15], (D,), jnp.float32, -0.5, 0.5), -0.5, 0.5)
    w_cross_q = centred(key_list[16], (D, HH), D ** -0.5, 0.1875, ((1, 2),))
    w_cross_out_t = centred(key_list[17], (D, HH), HH ** -0.5, 0.1875, ((1, 2),))
    gain_cross = jnp.clip(1.0 + 0.15 * jax.random.normal(key_list[18], (D,), jnp.float32), 0.25, 1.75)
    bias_cross = jnp.clip(jax.random.uniform(key_list[19], (D,), jnp.float32, -0.5, 0.5), -0.5, 0.5)
    return dict(queries=queries, new_keys=new_keys, new_values=new_values, sink_keys=sink_keys, sink_values=sink_values, pool_keys=pool_keys, pool_values=pool_values, block_ids=block_ids, cache_lengths=cache_lengths, cross_keys=cross_keys, cross_values=cross_values, enc_lengths=enc_lengths, hidden=hidden, w_out_t=w_out_t, gain_self=gain_self, bias_self=bias_self, w_cross_q=w_cross_q, w_cross_out_t=w_cross_out_t, gain_cross=gain_cross, bias_cross=bias_cross)


masked_score = -1e+30
norm_eps = 1e-05

def attend(query_rows, key_rows, value_rows, visible):
    row_count = query_rows.shape[0]
    key_count = key_rows.shape[0]
    query_heads = query_rows.astype(jnp.float32).reshape(row_count, H, HD)
    key_heads = key_rows.astype(jnp.float32).reshape(key_count, H, HD)
    value_heads = value_rows.astype(jnp.float32).reshape(key_count, H, HD)
    scores = jnp.einsum('qhd,khd->hqk', query_heads, key_heads) * HD ** (-0.5)
    scores = jnp.where(visible[None], scores, masked_score)
    row_top = lax.optimization_barrier(jnp.max(scores, axis=-1, keepdims=True))
    weights = jnp.where(visible[None], jnp.exp(scores - row_top), 0.0)
    row_total = lax.optimization_barrier(jnp.sum(weights, axis=-1))
    probabilities = lax.optimization_barrier(weights.astype(jnp.bfloat16)).astype(jnp.float32)
    summed = jnp.einsum('hqk,khd->qhd', probabilities, value_heads)
    result = summed / jnp.transpose(row_total)[:, :, None]
    return result.reshape(row_count, H * HD)

def layer_norm(pre_norm, gain_vec, bias_vec):
    row_mean = lax.optimization_barrier(jnp.mean(pre_norm, axis=-1, keepdims=True))
    centered = pre_norm - row_mean
    row_var = lax.optimization_barrier(jnp.mean(centered * centered, axis=-1, keepdims=True))
    return centered * lax.rsqrt(row_var + norm_eps) * gain_vec + bias_vec

def reference(queries, new_keys, new_values, sink_keys, sink_values, pool_keys, pool_values, block_ids, cache_lengths, cross_keys, cross_values, enc_lengths, hidden, w_out_t, gain_self, bias_self, w_cross_q, w_cross_out_t, gain_cross, bias_cross):

    def per_request(request):
        row_start = request * SPAN
        query_rows = lax.dynamic_slice_in_dim(queries, row_start, SPAN, 0)
        own_keys = lax.dynamic_slice_in_dim(new_keys, row_start, SPAN, 0)
        own_values = lax.dynamic_slice_in_dim(new_values, row_start, SPAN, 0)
        hidden_rows = lax.dynamic_slice_in_dim(hidden, row_start, SPAN, 0)
        cache_len = cache_lengths[request]
        slot_range = jnp.arange(SLOTS, dtype=jnp.int32)
        rows_held = ((request + 1 + slot_range) % REQS).astype(jnp.int32)
        block_keys = pool_keys[rows_held, slot_range].reshape(SLOTS * BS, H * HD)
        block_values = pool_values[rows_held, slot_range].reshape(SLOTS * BS, H * HD)
        held_ids = block_ids[rows_held, slot_range]
        positions = (held_ids[:, None] * BS + jnp.arange(BS, dtype=jnp.int32)[None, :]).reshape(-1)
        query_pos = cache_len + jnp.arange(SPAN, dtype=jnp.int32)
        window_vis = (positions[None, :] > query_pos[:, None] - WINDOW) & (positions[None, :] < cache_len)
        token_range = jnp.arange(SPAN, dtype=jnp.int32)
        own_vis = token_range[None, :] <= token_range[:, None]
        sink_vis = jnp.ones((SPAN, SINK), dtype=bool)
        all_keys = jnp.concatenate([sink_keys[request], block_keys, own_keys], axis=0)
        all_values = jnp.concatenate([sink_values[request], block_values, own_values], axis=0)
        all_vis = jnp.concatenate([sink_vis, window_vis, own_vis], axis=1)
        attended = attend(query_rows, all_keys, all_values, all_vis).astype(jnp.bfloat16)
        self_proj = jnp.dot(attended, w_out_t.T, preferred_element_type=jnp.float32)
        normed = layer_norm(hidden_rows.astype(jnp.float32) + self_proj, gain_self, bias_self).astype(jnp.bfloat16)
        cross_query = jnp.dot(normed, w_cross_q, preferred_element_type=jnp.float32).astype(jnp.bfloat16)
        enc_vis = jnp.broadcast_to(jnp.arange(ENC, dtype=jnp.int32)[None, :] < enc_lengths[request], (SPAN, ENC))
        context = attend(cross_query, cross_keys[request], cross_values[request], enc_vis).astype(jnp.bfloat16)
        cross_proj = jnp.dot(context, w_cross_out_t.T, preferred_element_type=jnp.float32)
        return layer_norm(normed.astype(jnp.float32) + cross_proj, gain_cross, bias_cross).astype(jnp.bfloat16)
    stacked = lax.map(per_request, jnp.arange(REQS, dtype=jnp.int32))
    return stacked.reshape(TOKENS, D)
```

```python
import jax
import jax.numpy as jnp
from jax import lax
from jax.sharding import PartitionSpec as P

HD = 64
WINDOW = 4096


masked_score = -1e30
norm_eps = 1e-05


def passed_along(block, axis, distance):
    devices = range(lax.axis_size(axis))
    route = [((i - distance) % len(devices), i) for i in devices]
    return lax.ppermute(block, axis, route)


def partial_block(query_rows, key_rows, value_rows, visible):
    row_count = query_rows.shape[0]
    key_count = key_rows.shape[0]
    head_count = query_rows.shape[1] // HD
    query_heads = query_rows.reshape(row_count, head_count, HD)
    key_heads = key_rows.reshape(key_count, head_count, HD)
    value_heads = value_rows.reshape(key_count, head_count, HD)
    scores = jnp.einsum(
        "qhd,khd->hqk", query_heads, key_heads, preferred_element_type=jnp.float32
    ) * HD ** (-0.5)
    scores = jnp.where(visible[None], scores, masked_score)
    row_top = jnp.max(scores, axis=-1)
    weights = jnp.where(visible[None], jnp.exp(scores - row_top[..., None]), 0.0)
    row_total = jnp.sum(weights, axis=-1)
    summed = jnp.einsum(
        "hqk,khd->hqd",
        weights.astype(jnp.bfloat16),
        value_heads,
        preferred_element_type=jnp.float32,
    )
    return (summed, row_top, row_total)


def combine(current, incoming):
    out_a, top_a, total_a = current
    out_b, top_b, total_b = incoming
    new_top = jnp.maximum(top_a, top_b)
    scale_a = jnp.exp(top_a - new_top)
    scale_b = jnp.exp(top_b - new_top)
    return (
        out_a * scale_a[..., None] + out_b * scale_b[..., None],
        new_top,
        total_a * scale_a + total_b * scale_b,
    )


def window_visible(block_number, cache_len, row_count, block_rows):
    positions = block_number * block_rows + jnp.arange(block_rows, dtype=jnp.int32)
    query_pos = cache_len + jnp.arange(row_count, dtype=jnp.int32)
    return (positions[None, :] > query_pos[:, None] - WINDOW) & (positions[None, :] < cache_len)


def finish_heads(merged):
    summed, row_top, row_total = merged
    result = summed / row_total[..., None]
    head_count, row_count, head_size = result.shape
    return (
        jnp.transpose(result, (1, 0, 2))
        .reshape(row_count, head_count * head_size)
        .astype(jnp.bfloat16)
    )


def head_whole(projected):
    part = projected.astype(jnp.bfloat16)
    other = lax.ppermute(part, "head", [(0, 1), (1, 0)])
    return part.astype(jnp.float32) + other.astype(jnp.float32)


def full_norm(pre_norm, gain_vec, bias_vec):
    row_mean = jnp.mean(pre_norm, axis=-1, keepdims=True)
    centered = pre_norm - row_mean
    row_var = jnp.mean(centered * centered, axis=-1, keepdims=True)
    return centered * lax.rsqrt(row_var + norm_eps) * gain_vec + bias_vec


def project_back(rows_in, weight_t):
    return lax.dot_general(
        rows_in, weight_t, (((1,), (1,)), ((), ())), preferred_element_type=jnp.float32
    )


def per_device(
    queries,
    new_keys,
    new_values,
    sink_keys,
    sink_values,
    pool_keys,
    pool_values,
    block_ids,
    cache_lengths,
    cross_keys,
    cross_values,
    enc_lengths,
    hidden,
    w_out_t,
    gain_self,
    bias_self,
    w_cross_q,
    w_cross_out_t,
    gain_cross,
    bias_cross,
):
    device = lax.axis_index("blk")
    blk_count = lax.axis_size("blk")
    span_rows = queries.shape[0]
    slot_count = pool_keys.shape[1]
    block_rows = pool_keys.shape[2]
    sink_count = sink_keys.shape[1]
    own_length = lax.dynamic_index_in_dim(cache_lengths, device, keepdims=False)
    local_keys = jnp.concatenate([sink_keys[0], new_keys], axis=0)
    local_values = jnp.concatenate([sink_values[0], new_values], axis=0)
    token_range = jnp.arange(span_rows, dtype=jnp.int32)
    local_visible = jnp.concatenate(
        [
            jnp.ones((span_rows, sink_count), dtype=bool),
            token_range[None, :] <= token_range[:, None],
        ],
        axis=1,
    )
    merged = partial_block(queries, local_keys, local_values, local_visible)
    for slot_step in range(1, slot_count + 1):
        key_block, value_block = passed_along(
            (pool_keys[0, slot_step - 1], pool_values[0, slot_step - 1]), "blk", -slot_step
        )
        holder = (device + slot_step) % blk_count
        held_block = lax.dynamic_index_in_dim(block_ids[:, slot_step - 1], holder, keepdims=False)
        visible = window_visible(held_block, own_length, span_rows, block_rows)
        merged = combine(merged, partial_block(queries, key_block, value_block, visible))
    attended = finish_heads(merged)
    self_proj = project_back(attended, w_out_t)
    head_index = lax.axis_index("head")
    head_width = hidden.shape[1]
    col_start = head_index * head_width
    own_cols = lax.dynamic_slice_in_dim(self_proj, col_start, head_width, 1) + hidden.astype(
        jnp.float32
    )
    with_residual = lax.dynamic_update_slice_in_dim(self_proj, own_cols, col_start, 1)
    pre_full = head_whole(with_residual)
    normed_full = full_norm(pre_full, gain_self, bias_self).astype(jnp.bfloat16)
    cross_query = jnp.dot(normed_full, w_cross_q, preferred_element_type=jnp.float32).astype(
        jnp.bfloat16
    )
    enc_count = cross_keys.shape[1]
    enc_length = enc_lengths[0]
    enc_visible = jnp.broadcast_to(
        jnp.arange(enc_count, dtype=jnp.int32)[None, :] < enc_length, (span_rows, enc_count)
    )
    context = finish_heads(partial_block(cross_query, cross_keys[0], cross_values[0], enc_visible))
    cross_proj = project_back(context, w_cross_out_t)
    own_normed = lax.dynamic_slice_in_dim(normed_full, col_start, head_width, 1).astype(jnp.float32)
    own_cross = lax.dynamic_slice_in_dim(cross_proj, col_start, head_width, 1) + own_normed
    cross_residual = lax.dynamic_update_slice_in_dim(cross_proj, own_cross, col_start, 1)
    second_full = head_whole(cross_residual)
    full_out = full_norm(second_full, gain_cross, bias_cross).astype(jnp.bfloat16)
    layer_out = lax.dynamic_slice_in_dim(full_out, col_start, head_width, 1)
    return layer_out


def solution(mesh):
    placed = (
        P("blk", "head"),
        P("blk", "head"),
        P("blk", "head"),
        P("blk", None, "head"),
        P("blk", None, "head"),
        P("blk", None, None, "head"),
        P("blk", None, None, "head"),
        P(),
        P(),
        P("blk", None, "head"),
        P("blk", None, "head"),
        P("blk"),
        P("blk", "head"),
        P(None, "head"),
        P(),
        P(),
        P(None, "head"),
        P(None, "head"),
        P(),
        P(),
    )
    return jax.shard_map(
        per_device, mesh=mesh, in_specs=placed, out_specs=P("blk", "head"), check_vma=False
    )
```

```python
import jax
import jax.numpy as jnp
from jax import lax
from jax.sharding import PartitionSpec as P

HD = 64
WINDOW = 4096


masked_score = -1e30
norm_eps = 1e-05


def passed_along(block, axis, distance):
    devices = range(lax.axis_size(axis))
    route = [((i - distance) % len(devices), i) for i in devices]
    return lax.ppermute(block, axis, route)


def partial_block(query_rows, key_rows, value_rows, visible):
    row_count = query_rows.shape[0]
    key_count = key_rows.shape[0]
    head_count = query_rows.shape[1] // HD
    query_heads = query_rows.reshape(row_count, head_count, HD)
    key_heads = key_rows.reshape(key_count, head_count, HD)
    value_heads = value_rows.reshape(key_count, head_count, HD)
    scores = jnp.einsum(
        "qhd,khd->hqk", query_heads, key_heads, preferred_element_type=jnp.float32
    ) * HD ** (-0.5)
    scores = jnp.where(visible[None], scores, masked_score)
    row_top = jnp.max(scores, axis=-1)
    weights = jnp.where(visible[None], jnp.exp(scores - row_top[..., None]), 0.0)
    row_total = jnp.sum(weights, axis=-1)
    summed = jnp.einsum(
        "hqk,khd->hqd",
        weights.astype(jnp.bfloat16),
        value_heads,
        preferred_element_type=jnp.float32,
    )
    return (summed, row_top, row_total)


def combine(current, incoming):
    out_a, top_a, total_a = current
    out_b, top_b, total_b = incoming
    new_top = jnp.maximum(top_a, top_b)
    scale_a = jnp.exp(top_a - new_top)
    scale_b = jnp.exp(top_b - new_top)
    return (
        out_a * scale_a[..., None] + out_b * scale_b[..., None],
        new_top,
        total_a * scale_a + total_b * scale_b,
    )


def window_visible(block_number, cache_len, row_count, block_rows):
    positions = block_number * block_rows + jnp.arange(block_rows, dtype=jnp.int32)
    query_pos = cache_len + jnp.arange(row_count, dtype=jnp.int32)
    return (positions[None, :] > query_pos[:, None] - WINDOW) & (positions[None, :] < cache_len)


def finish_heads(merged):
    summed, row_top, row_total = merged
    result = summed / row_total[..., None]
    head_count, row_count, head_size = result.shape
    return (
        jnp.transpose(result, (1, 0, 2))
        .reshape(row_count, head_count * head_size)
        .astype(jnp.bfloat16)
    )


def head_whole(projected):
    part = projected.astype(jnp.bfloat16)
    other = lax.ppermute(part, "head", [(0, 1), (1, 0)])
    return part.astype(jnp.float32) + other.astype(jnp.float32)


def full_norm(pre_norm, gain_vec, bias_vec):
    row_mean = jnp.mean(pre_norm, axis=-1, keepdims=True)
    centered = pre_norm - row_mean
    row_var = jnp.mean(centered * centered, axis=-1, keepdims=True)
    return centered * lax.rsqrt(row_var + norm_eps) * gain_vec + bias_vec


def project_back(rows_in, weight_t):
    return lax.dot_general(
        rows_in, weight_t, (((1,), (1,)), ((), ())), preferred_element_type=jnp.float32
    )


def per_device(
    queries,
    new_keys,
    new_values,
    sink_keys,
    sink_values,
    pool_keys,
    pool_values,
    block_ids,
    cache_lengths,
    cross_keys,
    cross_values,
    enc_lengths,
    hidden,
    w_out_t,
    gain_self,
    bias_self,
    w_cross_q,
    w_cross_out_t,
    gain_cross,
    bias_cross,
):
    device = lax.axis_index("blk")
    blk_count = lax.axis_size("blk")
    span_rows = queries.shape[0]
    slot_count = pool_keys.shape[1]
    block_rows = pool_keys.shape[2]
    sink_count = sink_keys.shape[1]
    own_length = lax.dynamic_index_in_dim(cache_lengths, device, keepdims=False)
    local_keys = jnp.concatenate([sink_keys[0], new_keys], axis=0)
    local_values = jnp.concatenate([sink_values[0], new_values], axis=0)
    token_range = jnp.arange(span_rows, dtype=jnp.int32)
    local_visible = jnp.concatenate(
        [
            jnp.ones((span_rows, sink_count), dtype=bool),
            token_range[None, :] <= token_range[:, None],
        ],
        axis=1,
    )
    merged = partial_block(queries, local_keys, local_values, local_visible)
    travelling = queries
    for slot_step in range(1, slot_count + 1):
        travelling = passed_along(travelling, "blk", 1)
        asker = (device - slot_step) % blk_count
        asker_length = lax.dynamic_index_in_dim(cache_lengths, asker, keepdims=False)
        held_block = lax.dynamic_index_in_dim(block_ids[:, slot_step - 1], device, keepdims=False)
        visible = window_visible(held_block, asker_length, span_rows, block_rows)
        summed, row_top, row_total = partial_block(
            travelling, pool_keys[0, slot_step - 1], pool_values[0, slot_step - 1], visible
        )
        summed_home = passed_along(summed.astype(jnp.bfloat16), "blk", -slot_step)
        stats_home = passed_along(jnp.stack([row_top, row_total]), "blk", -slot_step)
        merged = combine(
            merged, (summed_home.astype(jnp.float32), stats_home[0], stats_home[1])
        )
    attended = finish_heads(merged)
    self_proj = project_back(attended, w_out_t)
    head_index = lax.axis_index("head")
    head_width = hidden.shape[1]
    col_start = head_index * head_width
    own_cols = lax.dynamic_slice_in_dim(self_proj, col_start, head_width, 1) + hidden.astype(
        jnp.float32
    )
    with_residual = lax.dynamic_update_slice_in_dim(self_proj, own_cols, col_start, 1)
    pre_full = head_whole(with_residual)
    normed_full = full_norm(pre_full, gain_self, bias_self).astype(jnp.bfloat16)
    cross_query = jnp.dot(normed_full, w_cross_q, preferred_element_type=jnp.float32).astype(
        jnp.bfloat16
    )
    enc_count = cross_keys.shape[1]
    enc_length = enc_lengths[0]
    enc_visible = jnp.broadcast_to(
        jnp.arange(enc_count, dtype=jnp.int32)[None, :] < enc_length, (span_rows, enc_count)
    )
    context = finish_heads(partial_block(cross_query, cross_keys[0], cross_values[0], enc_visible))
    cross_proj = project_back(context, w_cross_out_t)
    own_normed = lax.dynamic_slice_in_dim(normed_full, col_start, head_width, 1).astype(jnp.float32)
    own_cross = lax.dynamic_slice_in_dim(cross_proj, col_start, head_width, 1) + own_normed
    cross_residual = lax.dynamic_update_slice_in_dim(cross_proj, own_cross, col_start, 1)
    second_full = head_whole(cross_residual)
    full_out = full_norm(second_full, gain_cross, bias_cross).astype(jnp.bfloat16)
    layer_out = lax.dynamic_slice_in_dim(full_out, col_start, head_width, 1)
    return layer_out


def solution(mesh):
    placed = (
        P("blk", "head"),
        P("blk", "head"),
        P("blk", "head"),
        P("blk", None, "head"),
        P("blk", None, "head"),
        P("blk", None, None, "head"),
        P("blk", None, None, "head"),
        P(),
        P(),
        P("blk", None, "head"),
        P("blk", None, "head"),
        P("blk"),
        P("blk", "head"),
        P(None, "head"),
        P(),
        P(),
        P(None, "head"),
        P(None, "head"),
        P(),
        P(),
    )
    return jax.shard_map(
        per_device, mesh=mesh, in_specs=placed, out_specs=P("blk", "head"), check_vma=False
    )
```

```python
import jax
import jax.numpy as jnp
from jax import lax
from jax.sharding import PartitionSpec as P

HD = 64
WINDOW = 4096


masked_score = -1e30
top_floor = -1e20
norm_eps = 1e-05


def passed_along(block, axis, distance):
    devices = range(lax.axis_size(axis))
    route = [((i - distance) % len(devices), i) for i in devices]
    return lax.ppermute(block, axis, route)


def partial_block(query_rows, key_rows, value_rows, visible):
    row_count = query_rows.shape[0]
    key_count = key_rows.shape[0]
    head_count = query_rows.shape[1] // HD
    query_heads = query_rows.reshape(row_count, head_count, HD)
    key_heads = key_rows.reshape(key_count, head_count, HD)
    value_heads = value_rows.reshape(key_count, head_count, HD)
    scores = jnp.einsum(
        "qhd,khd->hqk", query_heads, key_heads, preferred_element_type=jnp.float32
    ) * HD ** (-0.5)
    scores = scores + jnp.where(visible, 0.0, masked_score)[None]
    row_top = jnp.maximum(jnp.max(scores, axis=-1), top_floor)
    weights = jnp.exp(scores - row_top[..., None])
    row_total = jnp.sum(weights, axis=-1)
    summed = jnp.einsum(
        "hqk,khd->hqd",
        weights.astype(jnp.bfloat16),
        value_heads,
        preferred_element_type=jnp.float32,
    )
    return (summed, row_top, row_total)


def combine(current, incoming):
    out_a, top_a, total_a = current
    out_b, top_b, total_b = incoming
    new_top = jnp.maximum(top_a, top_b)
    scale_a = jnp.exp(top_a - new_top)
    scale_b = jnp.exp(top_b - new_top)
    return (
        out_a * scale_a[..., None] + out_b * scale_b[..., None],
        new_top,
        total_a * scale_a + total_b * scale_b,
    )


def window_visible(block_number, cache_len, row_count, block_rows):
    positions = block_number * block_rows + jnp.arange(block_rows, dtype=jnp.int32)
    query_pos = cache_len + jnp.arange(row_count, dtype=jnp.int32)
    return (positions[None, :] > query_pos[:, None] - WINDOW) & (positions[None, :] < cache_len)


def finish_heads(merged):
    summed, row_top, row_total = merged
    result = summed / row_total[..., None]
    head_count, row_count, head_size = result.shape
    return (
        jnp.transpose(result, (1, 0, 2))
        .reshape(row_count, head_count * head_size)
        .astype(jnp.bfloat16)
    )


def head_whole(projected):
    part = projected.astype(jnp.bfloat16)
    other = lax.ppermute(part, "head", [(0, 1), (1, 0)])
    return part.astype(jnp.float32) + other.astype(jnp.float32)


def full_norm(pre_norm, gain_vec, bias_vec):
    row_mean = jnp.mean(pre_norm, axis=-1, keepdims=True)
    centered = pre_norm - row_mean
    row_var = jnp.mean(centered * centered, axis=-1, keepdims=True)
    return centered * lax.rsqrt(row_var + norm_eps) * gain_vec + bias_vec


def project_back(rows_in, weight_t):
    return lax.dot_general(
        rows_in, weight_t, (((1,), (1,)), ((), ())), preferred_element_type=jnp.float32
    )


def per_device(
    queries,
    new_keys,
    new_values,
    sink_keys,
    sink_values,
    pool_keys,
    pool_values,
    block_ids,
    cache_lengths,
    cross_keys,
    cross_values,
    enc_lengths,
    hidden,
    w_out_t,
    gain_self,
    bias_self,
    w_cross_q,
    w_cross_out_t,
    gain_cross,
    bias_cross,
):
    device = lax.axis_index("blk")
    blk_count = lax.axis_size("blk")
    span_rows = queries.shape[0]
    slot_count = pool_keys.shape[1]
    block_rows = pool_keys.shape[2]
    sink_count = sink_keys.shape[1]
    own_length = lax.dynamic_index_in_dim(cache_lengths, device, keepdims=False)
    local_keys = jnp.concatenate([sink_keys[0], new_keys], axis=0)
    local_values = jnp.concatenate([sink_values[0], new_values], axis=0)
    token_range = jnp.arange(span_rows, dtype=jnp.int32)
    local_visible = jnp.concatenate(
        [
            jnp.ones((span_rows, sink_count), dtype=bool),
            token_range[None, :] <= token_range[:, None],
        ],
        axis=1,
    )
    merged = partial_block(queries, local_keys, local_values, local_visible)
    for slot_step in range(1, slot_count + 1):
        travelling = passed_along(queries, "blk", slot_step)
        asker = (device - slot_step) % blk_count
        asker_length = lax.dynamic_index_in_dim(cache_lengths, asker, keepdims=False)
        held_block = lax.dynamic_index_in_dim(block_ids[:, slot_step - 1], device, keepdims=False)
        visible = window_visible(held_block, asker_length, span_rows, block_rows)
        summed, row_top, row_total = partial_block(
            travelling, pool_keys[0, slot_step - 1], pool_values[0, slot_step - 1], visible
        )
        summed_home = passed_along(summed.astype(jnp.bfloat16), "blk", -slot_step)
        stats_home = passed_along(jnp.stack([row_top, row_total]), "blk", -slot_step)
        merged = combine(
            merged, (summed_home.astype(jnp.float32), stats_home[0], stats_home[1])
        )
    attended = finish_heads(merged)
    self_proj = project_back(attended, w_out_t)
    head_index = lax.axis_index("head")
    head_width = hidden.shape[1]
    col_start = head_index * head_width
    own_cols = lax.dynamic_slice_in_dim(self_proj, col_start, head_width, 1) + hidden.astype(
        jnp.float32
    )
    with_residual = lax.dynamic_update_slice_in_dim(self_proj, own_cols, col_start, 1)
    pre_full = head_whole(with_residual)
    normed_full = full_norm(pre_full, gain_self, bias_self).astype(jnp.bfloat16)
    cross_query = jnp.dot(normed_full, w_cross_q, preferred_element_type=jnp.float32).astype(
        jnp.bfloat16
    )
    enc_count = cross_keys.shape[1]
    enc_length = enc_lengths[0]
    enc_visible = jnp.broadcast_to(
        jnp.arange(enc_count, dtype=jnp.int32)[None, :] < enc_length, (span_rows, enc_count)
    )
    context = finish_heads(partial_block(cross_query, cross_keys[0], cross_values[0], enc_visible))
    cross_proj = project_back(context, w_cross_out_t)
    own_normed = lax.dynamic_slice_in_dim(normed_full, col_start, head_width, 1).astype(jnp.float32)
    own_cross = lax.dynamic_slice_in_dim(cross_proj, col_start, head_width, 1) + own_normed
    cross_residual = lax.dynamic_update_slice_in_dim(cross_proj, own_cross, col_start, 1)
    second_full = head_whole(cross_residual)
    full_out = full_norm(second_full, gain_cross, bias_cross).astype(jnp.bfloat16)
    layer_out = lax.dynamic_slice_in_dim(full_out, col_start, head_width, 1)
    return layer_out


def solution(mesh):
    placed = (
        P("blk", "head"),
        P("blk", "head"),
        P("blk", "head"),
        P("blk", None, "head"),
        P("blk", None, "head"),
        P("blk", None, None, "head"),
        P("blk", None, None, "head"),
        P(),
        P(),
        P("blk", None, "head"),
        P("blk", None, "head"),
        P("blk"),
        P("blk", "head"),
        P(None, "head"),
        P(),
        P(),
        P(None, "head"),
        P(None, "head"),
        P(),
        P(),
    )
    return jax.shard_map(
        per_device, mesh=mesh, in_specs=placed, out_specs=P("blk", "head"), check_vma=False
    )
```

```python
import jax
import jax.numpy as jnp
from jax import lax
from jax.experimental import pallas as pl
from jax.experimental.pallas import tpu as pltpu
from jax.sharding import PartitionSpec as P

HD = 64
WINDOW = 4096


masked_score = -1e30
top_floor = -1e20
norm_eps = 1e-05


def passed_along(block, axis, distance):
    devices = range(lax.axis_size(axis))
    route = [((i - distance) % len(devices), i) for i in devices]
    return lax.ppermute(block, axis, route)


def partial_block(query_rows, key_rows, value_rows, visible):
    row_count = query_rows.shape[0]
    key_count = key_rows.shape[0]
    head_count = query_rows.shape[1] // HD
    query_heads = query_rows.reshape(row_count, head_count, HD)
    key_heads = key_rows.reshape(key_count, head_count, HD)
    value_heads = value_rows.reshape(key_count, head_count, HD)
    scores = jnp.einsum(
        "qhd,khd->hqk", query_heads, key_heads, preferred_element_type=jnp.float32
    ) * HD ** (-0.5)
    scores = scores + jnp.where(visible, 0.0, masked_score)[None]
    row_top = jnp.maximum(jnp.max(scores, axis=-1), top_floor)
    weights = jnp.exp(scores - row_top[..., None])
    row_total = jnp.sum(weights, axis=-1)
    summed = jnp.einsum(
        "hqk,khd->hqd",
        weights.astype(jnp.bfloat16),
        value_heads,
        preferred_element_type=jnp.float32,
    )
    return (summed, row_top, row_total)


def window_kernel(bounds_ref, q_ref, k_ref, v_ref, out_ref, stats_ref):
    row_count = q_ref.shape[0]
    key_count = k_ref.shape[0]
    head_count = q_ref.shape[1] // HD
    low = bounds_ref[0]
    high = bounds_ref[1]
    row = lax.broadcasted_iota(jnp.int32, (row_count, key_count), 0)
    col = lax.broadcasted_iota(jnp.int32, (row_count, key_count), 1)
    bias = jnp.where((col - row > low) & (col < high), 0.0, masked_score)
    for head in range(head_count):
        cols = slice(head * HD, (head + 1) * HD)
        scores = lax.dot_general(
            q_ref[:, cols], k_ref[:, cols], (((1,), (1,)), ((), ())),
            preferred_element_type=jnp.float32,
        ) * HD ** (-0.5) + bias
        top = jnp.maximum(jnp.max(scores, axis=1, keepdims=True), top_floor)
        weights = jnp.exp(scores - top)
        out_ref[:, cols] = jnp.dot(
            weights.astype(jnp.bfloat16), v_ref[:, cols], preferred_element_type=jnp.float32
        ).astype(out_ref.dtype)
        stats_ref[:, head : head + 1] = top
        stats_ref[:, head_count + head : head_count + head + 1] = jnp.sum(
            weights, axis=1, keepdims=True
        )


def window_partial(bounds, query_rows, pool_k, pool_v, slot):
    row_count, width = query_rows.shape
    key_count = pool_k.shape[1]
    head_count = width // HD
    whole = lambda i: (0, 0)
    in_slot = lambda i: (slot, 0, 0)
    return pl.pallas_call(
        window_kernel,
        grid=(1,),
        in_specs=[
            pl.BlockSpec(memory_space=pltpu.SMEM),
            pl.BlockSpec((row_count, width), whole),
            pl.BlockSpec((None, key_count, width), in_slot),
            pl.BlockSpec((None, key_count, width), in_slot),
        ],
        out_specs=[
            pl.BlockSpec((row_count, width), whole),
            pl.BlockSpec((row_count, 2 * head_count), whole),
        ],
        out_shape=[
            jax.ShapeDtypeStruct((row_count, width), jnp.bfloat16),
            jax.ShapeDtypeStruct((row_count, 2 * head_count), jnp.float32),
        ],
    )(bounds, query_rows, pool_k, pool_v)


def combine(current, incoming):
    out_a, top_a, total_a = current
    out_b, top_b, total_b = incoming
    new_top = jnp.maximum(top_a, top_b)
    scale_a = jnp.exp(top_a - new_top)
    scale_b = jnp.exp(top_b - new_top)
    return (
        out_a * scale_a[..., None] + out_b * scale_b[..., None],
        new_top,
        total_a * scale_a + total_b * scale_b,
    )


def window_visible(block_number, cache_len, row_count, block_rows):
    positions = block_number * block_rows + jnp.arange(block_rows, dtype=jnp.int32)
    query_pos = cache_len + jnp.arange(row_count, dtype=jnp.int32)
    return (positions[None, :] > query_pos[:, None] - WINDOW) & (positions[None, :] < cache_len)


def finish_heads(merged):
    summed, row_top, row_total = merged
    result = summed / row_total[..., None]
    head_count, row_count, head_size = result.shape
    return (
        jnp.transpose(result, (1, 0, 2))
        .reshape(row_count, head_count * head_size)
        .astype(jnp.bfloat16)
    )


def head_whole(projected):
    part = projected.astype(jnp.bfloat16)
    other = lax.ppermute(part, "head", [(0, 1), (1, 0)])
    return part.astype(jnp.float32) + other.astype(jnp.float32)


def full_norm(pre_norm, gain_vec, bias_vec):
    row_mean = jnp.mean(pre_norm, axis=-1, keepdims=True)
    centered = pre_norm - row_mean
    row_var = jnp.mean(centered * centered, axis=-1, keepdims=True)
    return centered * lax.rsqrt(row_var + norm_eps) * gain_vec + bias_vec


def project_back(rows_in, weight_t):
    return lax.dot_general(
        rows_in, weight_t, (((1,), (1,)), ((), ())), preferred_element_type=jnp.float32
    )


def per_device(
    queries,
    new_keys,
    new_values,
    sink_keys,
    sink_values,
    pool_keys,
    pool_values,
    block_ids,
    cache_lengths,
    cross_keys,
    cross_values,
    enc_lengths,
    hidden,
    w_out_t,
    gain_self,
    bias_self,
    w_cross_q,
    w_cross_out_t,
    gain_cross,
    bias_cross,
):
    device = lax.axis_index("blk")
    blk_count = lax.axis_size("blk")
    span_rows = queries.shape[0]
    slot_count = pool_keys.shape[1]
    block_rows = pool_keys.shape[2]
    sink_count = sink_keys.shape[1]
    own_length = lax.dynamic_index_in_dim(cache_lengths, device, keepdims=False)
    local_keys = jnp.concatenate([sink_keys[0], new_keys], axis=0)
    local_values = jnp.concatenate([sink_values[0], new_values], axis=0)
    token_range = jnp.arange(span_rows, dtype=jnp.int32)
    local_visible = jnp.concatenate(
        [
            jnp.ones((span_rows, sink_count), dtype=bool),
            token_range[None, :] <= token_range[:, None],
        ],
        axis=1,
    )
    local_summed, local_top, local_total = partial_block(
        queries, local_keys, local_values, local_visible
    )
    head_count = queries.shape[1] // HD
    merged = (jnp.transpose(local_summed, (1, 0, 2)), local_top.T, local_total.T)
    for slot_step in range(1, slot_count + 1):
        travelling = passed_along(queries, "blk", slot_step)
        asker = (device - slot_step) % blk_count
        asker_length = lax.dynamic_index_in_dim(cache_lengths, asker, keepdims=False)
        held_block = lax.dynamic_index_in_dim(block_ids[:, slot_step - 1], device, keepdims=False)
        block_start = held_block * block_rows
        bounds = jnp.stack([asker_length - WINDOW - block_start, asker_length - block_start])
        summed, stats = window_partial(bounds, travelling, pool_keys[0], pool_values[0], slot_step - 1)
        summed_home = passed_along(summed, "blk", -slot_step)
        stats_home = passed_along(stats, "blk", -slot_step)
        merged = combine(
            merged,
            (
                summed_home.astype(jnp.float32).reshape(span_rows, head_count, HD),
                stats_home[:, :head_count],
                stats_home[:, head_count:],
            ),
        )
    attended = (merged[0] / merged[2][..., None]).reshape(span_rows, -1).astype(jnp.bfloat16)
    self_proj = project_back(attended, w_out_t)
    head_index = lax.axis_index("head")
    head_width = hidden.shape[1]
    col_start = head_index * head_width
    own_cols = lax.dynamic_slice_in_dim(self_proj, col_start, head_width, 1) + hidden.astype(
        jnp.float32
    )
    with_residual = lax.dynamic_update_slice_in_dim(self_proj, own_cols, col_start, 1)
    pre_full = head_whole(with_residual)
    normed_full = full_norm(pre_full, gain_self, bias_self).astype(jnp.bfloat16)
    cross_query = jnp.dot(normed_full, w_cross_q, preferred_element_type=jnp.float32).astype(
        jnp.bfloat16
    )
    enc_count = cross_keys.shape[1]
    enc_length = enc_lengths[0]
    enc_visible = jnp.broadcast_to(
        jnp.arange(enc_count, dtype=jnp.int32)[None, :] < enc_length, (span_rows, enc_count)
    )
    context = finish_heads(partial_block(cross_query, cross_keys[0], cross_values[0], enc_visible))
    cross_proj = project_back(context, w_cross_out_t)
    own_normed = lax.dynamic_slice_in_dim(normed_full, col_start, head_width, 1).astype(jnp.float32)
    own_cross = lax.dynamic_slice_in_dim(cross_proj, col_start, head_width, 1) + own_normed
    cross_residual = lax.dynamic_update_slice_in_dim(cross_proj, own_cross, col_start, 1)
    second_full = head_whole(cross_residual)
    full_out = full_norm(second_full, gain_cross, bias_cross).astype(jnp.bfloat16)
    layer_out = lax.dynamic_slice_in_dim(full_out, col_start, head_width, 1)
    return layer_out


def solution(mesh):
    placed = (
        P("blk", "head"),
        P("blk", "head"),
        P("blk", "head"),
        P("blk", None, "head"),
        P("blk", None, "head"),
        P("blk", None, None, "head"),
        P("blk", None, None, "head"),
        P(),
        P(),
        P("blk", None, "head"),
        P("blk", None, "head"),
        P("blk"),
        P("blk", "head"),
        P(None, "head"),
        P(),
        P(),
        P(None, "head"),
        P(None, "head"),
        P(),
        P(),
    )
    return jax.shard_map(
        per_device, mesh=mesh, in_specs=placed, out_specs=P("blk", "head"), check_vma=False
    )
```

```python
import jax
import jax.numpy as jnp
from jax import lax
from jax.experimental import pallas as pl
from jax.experimental.pallas import tpu as pltpu
from jax.sharding import PartitionSpec as P

HD = 64
WINDOW = 4096


masked_score = -1e30
top_floor = -1e20
FAR = 1 << 30
norm_eps = 1e-05


def passed_along(block, axis, distance):
    devices = range(lax.axis_size(axis))
    route = [((i - distance) % len(devices), i) for i in devices]
    return lax.ppermute(block, axis, route)


def partial_block(query_rows, key_rows, value_rows, visible):
    row_count = query_rows.shape[0]
    key_count = key_rows.shape[0]
    head_count = query_rows.shape[1] // HD
    query_heads = query_rows.reshape(row_count, head_count, HD)
    key_heads = key_rows.reshape(key_count, head_count, HD)
    value_heads = value_rows.reshape(key_count, head_count, HD)
    scores = jnp.einsum(
        "qhd,khd->hqk", query_heads, key_heads, preferred_element_type=jnp.float32
    ) * HD ** (-0.5)
    scores = scores + jnp.where(visible, 0.0, masked_score)[None]
    row_top = jnp.maximum(jnp.max(scores, axis=-1), top_floor)
    weights = jnp.exp(scores - row_top[..., None])
    row_total = jnp.sum(weights, axis=-1)
    summed = jnp.einsum(
        "hqk,khd->hqd",
        weights.astype(jnp.bfloat16),
        value_heads,
        preferred_element_type=jnp.float32,
    )
    return (summed, row_top, row_total)


def window_kernel(bounds_ref, q_ref, k_ref, v_ref, out_ref, stats_ref):
    row_count = q_ref.shape[0]
    key_count = k_ref.shape[0]
    head_count = q_ref.shape[1] // HD
    always = bounds_ref[0]
    low = bounds_ref[1]
    upper = bounds_ref[2]
    high = bounds_ref[3]
    row = lax.broadcasted_iota(jnp.int32, (row_count, key_count), 0)
    col = lax.broadcasted_iota(jnp.int32, (row_count, key_count), 1)
    rel = col - row
    visible = (col < always) | ((rel > low) & (rel < upper) & (col < high))
    bias = jnp.where(visible, 0.0, masked_score)
    for head in range(head_count):
        cols = slice(head * HD, (head + 1) * HD)
        scores = lax.dot_general(
            q_ref[:, cols], k_ref[:, cols], (((1,), (1,)), ((), ())),
            preferred_element_type=jnp.float32,
        ) * HD ** (-0.5) + bias
        top = jnp.maximum(jnp.max(scores, axis=1, keepdims=True), top_floor)
        weights = jnp.exp(scores - top)
        out_ref[:, cols] = jnp.dot(
            weights.astype(jnp.bfloat16), v_ref[:, cols], preferred_element_type=jnp.float32
        ).astype(out_ref.dtype)
        stats_ref[:, head : head + 1] = top
        stats_ref[:, head_count + head : head_count + head + 1] = jnp.sum(
            weights, axis=1, keepdims=True
        )


def attention_partial(bounds, query_rows, key_rows, value_rows, out_dtype, slot=None):
    row_count, width = query_rows.shape
    key_count = key_rows.shape[-2]
    head_count = width // HD
    whole = lambda i: (0, 0)
    if slot is None:
        key_spec = pl.BlockSpec((key_count, width), whole)
    else:
        key_spec = pl.BlockSpec((None, key_count, width), lambda i: (slot, 0, 0))
    return pl.pallas_call(
        window_kernel,
        grid=(1,),
        in_specs=[
            pl.BlockSpec(memory_space=pltpu.SMEM),
            pl.BlockSpec((row_count, width), whole),
            key_spec,
            key_spec,
        ],
        out_specs=[
            pl.BlockSpec((row_count, width), whole),
            pl.BlockSpec((row_count, 2 * head_count), whole),
        ],
        out_shape=[
            jax.ShapeDtypeStruct((row_count, width), out_dtype),
            jax.ShapeDtypeStruct((row_count, 2 * head_count), jnp.float32),
        ],
    )(bounds, query_rows, key_rows, value_rows)


def merge_kernel(*refs):
    count = (len(refs) - 1) // 2
    summed_refs = refs[:count]
    stats_refs = refs[count : 2 * count]
    out_ref = refs[2 * count]
    head_count = stats_refs[0].shape[1] // 2
    for head in range(head_count):
        cols = slice(head * HD, (head + 1) * HD)
        tops = [stats[:, head : head + 1] for stats in stats_refs]
        top = tops[0]
        for other in tops[1:]:
            top = jnp.maximum(top, other)
        total = 0.0
        acc = 0.0
        for part in range(count):
            scale = jnp.exp(tops[part] - top)
            total = total + stats_refs[part][:, head_count + head : head_count + head + 1] * scale
            acc = acc + summed_refs[part][:, cols].astype(jnp.float32) * scale
        out_ref[:, cols] = (acc / total).astype(out_ref.dtype)


def merge_partials(partials):
    summed_list = [summed for summed, _ in partials]
    stats_list = [stats for _, stats in partials]
    operands = summed_list + stats_list
    row_count, width = summed_list[0].shape
    whole = lambda i: (0, 0)
    return pl.pallas_call(
        merge_kernel,
        grid=(1,),
        in_specs=[pl.BlockSpec(x.shape, whole) for x in operands],
        out_specs=pl.BlockSpec((row_count, width), whole),
        out_shape=jax.ShapeDtypeStruct((row_count, width), jnp.bfloat16),
    )(*operands)


def combine(current, incoming):
    out_a, top_a, total_a = current
    out_b, top_b, total_b = incoming
    new_top = jnp.maximum(top_a, top_b)
    scale_a = jnp.exp(top_a - new_top)
    scale_b = jnp.exp(top_b - new_top)
    return (
        out_a * scale_a[..., None] + out_b * scale_b[..., None],
        new_top,
        total_a * scale_a + total_b * scale_b,
    )


def window_visible(block_number, cache_len, row_count, block_rows):
    positions = block_number * block_rows + jnp.arange(block_rows, dtype=jnp.int32)
    query_pos = cache_len + jnp.arange(row_count, dtype=jnp.int32)
    return (positions[None, :] > query_pos[:, None] - WINDOW) & (positions[None, :] < cache_len)


def finish_heads(merged):
    summed, row_top, row_total = merged
    result = summed / row_total[..., None]
    head_count, row_count, head_size = result.shape
    return (
        jnp.transpose(result, (1, 0, 2))
        .reshape(row_count, head_count * head_size)
        .astype(jnp.bfloat16)
    )


def head_whole(projected):
    part = projected.astype(jnp.bfloat16)
    other = lax.ppermute(part, "head", [(0, 1), (1, 0)])
    return part.astype(jnp.float32) + other.astype(jnp.float32)


def full_norm(pre_norm, gain_vec, bias_vec):
    row_mean = jnp.mean(pre_norm, axis=-1, keepdims=True)
    centered = pre_norm - row_mean
    row_var = jnp.mean(centered * centered, axis=-1, keepdims=True)
    return centered * lax.rsqrt(row_var + norm_eps) * gain_vec + bias_vec


def project_back(rows_in, weight_t):
    return lax.dot_general(
        rows_in, weight_t, (((1,), (1,)), ((), ())), preferred_element_type=jnp.float32
    )


def per_device(
    queries,
    new_keys,
    new_values,
    sink_keys,
    sink_values,
    pool_keys,
    pool_values,
    block_ids,
    cache_lengths,
    cross_keys,
    cross_values,
    enc_lengths,
    hidden,
    w_out_t,
    gain_self,
    bias_self,
    w_cross_q,
    w_cross_out_t,
    gain_cross,
    bias_cross,
):
    device = lax.axis_index("blk")
    blk_count = lax.axis_size("blk")
    span_rows = queries.shape[0]
    slot_count = pool_keys.shape[1]
    block_rows = pool_keys.shape[2]
    sink_count = sink_keys.shape[1]
    own_length = lax.dynamic_index_in_dim(cache_lengths, device, keepdims=False)
    pad_rows = (-(sink_count + span_rows)) % 16
    pad_block = jnp.zeros((pad_rows, new_keys.shape[1]), new_keys.dtype)
    local_keys = jnp.concatenate([sink_keys[0], new_keys, pad_block], axis=0)
    local_values = jnp.concatenate([sink_values[0], new_values, pad_block], axis=0)
    local_bounds = jnp.array([sink_count, -FAR, sink_count + 1, FAR], jnp.int32)
    partials = [
        attention_partial(local_bounds, queries, local_keys, local_values, jnp.float32)
    ]
    for slot_step in range(1, slot_count + 1):
        travelling = passed_along(queries, "blk", slot_step)
        asker = (device - slot_step) % blk_count
        asker_length = lax.dynamic_index_in_dim(cache_lengths, asker, keepdims=False)
        held_block = lax.dynamic_index_in_dim(block_ids[:, slot_step - 1], device, keepdims=False)
        block_start = held_block * block_rows
        bounds = jnp.stack(
            [0, asker_length - WINDOW - block_start, FAR, asker_length - block_start]
        ).astype(jnp.int32)
        summed, stats = attention_partial(
            bounds, travelling, pool_keys[0], pool_values[0], jnp.bfloat16, slot_step - 1
        )
        partials.append(
            (passed_along(summed, "blk", -slot_step), passed_along(stats, "blk", -slot_step))
        )
    attended = merge_partials(partials)
    self_proj = project_back(attended, w_out_t)
    head_index = lax.axis_index("head")
    head_width = hidden.shape[1]
    col_start = head_index * head_width
    own_cols = lax.dynamic_slice_in_dim(self_proj, col_start, head_width, 1) + hidden.astype(
        jnp.float32
    )
    with_residual = lax.dynamic_update_slice_in_dim(self_proj, own_cols, col_start, 1)
    pre_full = head_whole(with_residual)
    normed_full = full_norm(pre_full, gain_self, bias_self).astype(jnp.bfloat16)
    cross_query = jnp.dot(normed_full, w_cross_q, preferred_element_type=jnp.float32).astype(
        jnp.bfloat16
    )
    enc_bounds = jnp.stack([0, -FAR, FAR, enc_lengths[0]]).astype(jnp.int32)
    context = merge_partials(
        [attention_partial(enc_bounds, cross_query, cross_keys[0], cross_values[0], jnp.float32)]
    )
    cross_proj = project_back(context, w_cross_out_t)
    own_normed = lax.dynamic_slice_in_dim(normed_full, col_start, head_width, 1).astype(jnp.float32)
    own_cross = lax.dynamic_slice_in_dim(cross_proj, col_start, head_width, 1) + own_normed
    cross_residual = lax.dynamic_update_slice_in_dim(cross_proj, own_cross, col_start, 1)
    second_full = head_whole(cross_residual)
    full_out = full_norm(second_full, gain_cross, bias_cross).astype(jnp.bfloat16)
    layer_out = lax.dynamic_slice_in_dim(full_out, col_start, head_width, 1)
    return layer_out


def solution(mesh):
    placed = (
        P("blk", "head"),
        P("blk", "head"),
        P("blk", "head"),
        P("blk", None, "head"),
        P("blk", None, "head"),
        P("blk", None, None, "head"),
        P("blk", None, None, "head"),
        P(),
        P(),
        P("blk", None, "head"),
        P("blk", None, "head"),
        P("blk"),
        P("blk", "head"),
        P(None, "head"),
        P(),
        P(),
        P(None, "head"),
        P(None, "head"),
        P(),
        P(),
    )
    return jax.shard_map(
        per_device, mesh=mesh, in_specs=placed, out_specs=P("blk", "head"), check_vma=False
    )
```

```python
import jax
import jax.numpy as jnp
from jax import lax
from jax.experimental import pallas as pl
from jax.experimental.pallas import tpu as pltpu
from jax.sharding import PartitionSpec as P

HD = 64
WINDOW = 4096


masked_score = -1e30
top_floor = -1e20
FAR = 1 << 30
norm_eps = 1e-05


def passed_along(block, axis, distance):
    devices = range(lax.axis_size(axis))
    route = [((i - distance) % len(devices), i) for i in devices]
    return lax.ppermute(block, axis, route)


def partial_block(query_rows, key_rows, value_rows, visible):
    row_count = query_rows.shape[0]
    key_count = key_rows.shape[0]
    head_count = query_rows.shape[1] // HD
    query_heads = query_rows.reshape(row_count, head_count, HD)
    key_heads = key_rows.reshape(key_count, head_count, HD)
    value_heads = value_rows.reshape(key_count, head_count, HD)
    scores = jnp.einsum(
        "qhd,khd->hqk", query_heads, key_heads, preferred_element_type=jnp.float32
    ) * HD ** (-0.5)
    scores = scores + jnp.where(visible, 0.0, masked_score)[None]
    row_top = jnp.maximum(jnp.max(scores, axis=-1), top_floor)
    weights = jnp.exp(scores - row_top[..., None])
    row_total = jnp.sum(weights, axis=-1)
    summed = jnp.einsum(
        "hqk,khd->hqd",
        weights.astype(jnp.bfloat16),
        value_heads,
        preferred_element_type=jnp.float32,
    )
    return (summed, row_top, row_total)


def split_three(values):
    high = values.astype(jnp.bfloat16).astype(jnp.float32)
    rest = values - high
    middle = rest.astype(jnp.bfloat16).astype(jnp.float32)
    low = (rest - middle).astype(jnp.bfloat16).astype(jnp.float32)
    return (high, middle, low)


def window_kernel(bounds_ref, q_ref, k_ref, v_ref, *rest):
    out_ref = rest[-1]
    row_count, width = q_ref.shape
    key_count = k_ref.shape[0]
    head_count = width // HD
    always = bounds_ref[0]
    low = bounds_ref[1]
    upper = bounds_ref[2]
    high = bounds_ref[3]
    row = lax.broadcasted_iota(jnp.int32, (row_count, key_count), 0)
    col = lax.broadcasted_iota(jnp.int32, (row_count, key_count), 1)
    rel = col - row
    visible = (col < always) | ((rel > low) & (rel < upper) & (col < high))
    bias = jnp.where(visible, 0.0, masked_score)
    lane = lax.broadcasted_iota(jnp.int32, (row_count, 128), 1)
    first_half = lane < HD
    stats = jnp.zeros((row_count, 128), jnp.float32)
    for pair in range(width // 128):
        cols = slice(pair * 128, (pair + 1) * 128)
        q_pair = q_ref[:, cols]
        k_pair = k_ref[:, cols]
        v_pair = v_ref[:, cols]
        out_tile = jnp.zeros((row_count, 128), jnp.float32)
        for half in range(2):
            head = 2 * pair + half
            mine = first_half if half == 0 else jnp.logical_not(first_half)
            q_head = jnp.where(mine, q_pair, jnp.zeros_like(q_pair))
            scores = lax.dot_general(
                q_head, k_pair, (((1,), (1,)), ((), ())), preferred_element_type=jnp.float32
            ) * HD ** (-0.5) + bias
            top = jnp.maximum(jnp.max(scores, axis=1, keepdims=True), top_floor)
            weights = jnp.exp(scores - top)
            total = jnp.sum(weights, axis=1, keepdims=True)
            summed = jnp.dot(
                weights.astype(jnp.bfloat16), v_pair, preferred_element_type=jnp.float32
            )
            out_tile = jnp.where(mine, summed, out_tile)
            for piece, part in enumerate(split_three(top) + split_three(total)):
                stats = jnp.where(lane == piece * head_count + head, part, stats)
        out_ref[:, cols] = out_tile.astype(out_ref.dtype)
    out_ref[:, width : width + 128] = stats.astype(out_ref.dtype)


def attention_partial(bounds, query_rows, key_rows, value_rows, out_dtype, slot=None, after=None):
    row_count, width = query_rows.shape
    key_count = key_rows.shape[-2]
    whole = lambda i: (0, 0)
    if slot is None:
        key_spec = pl.BlockSpec((key_count, width), whole)
    else:
        key_spec = pl.BlockSpec((None, key_count, width), lambda i: (slot, 0, 0))
    operands = [bounds, query_rows, key_rows, value_rows]
    in_specs = [
        pl.BlockSpec(memory_space=pltpu.SMEM),
        pl.BlockSpec((row_count, width), whole),
        key_spec,
        key_spec,
    ]
    if after is not None:
        operands.append(after)
        in_specs.append(pl.BlockSpec(memory_space=pl.ANY))
    return pl.pallas_call(
        window_kernel,
        grid=(1,),
        in_specs=in_specs,
        out_specs=pl.BlockSpec((row_count, width + 128), whole),
        out_shape=jax.ShapeDtypeStruct((row_count, width + 128), out_dtype),
    )(*operands)


def merge_kernel(*refs):
    part_refs = refs[:-1]
    out_ref = refs[-1]
    row_count, width = out_ref.shape
    head_count = width // HD
    tops = []
    totals = []
    for ref in part_refs:
        stats = ref[:, width : width + 128].astype(jnp.float32)
        piece = lambda k: stats[:, k * head_count : (k + 1) * head_count]
        tops.append(piece(0) + piece(1) + piece(2))
        totals.append(piece(3) + piece(4) + piece(5))
    top = tops[0]
    for other in tops[1:]:
        top = jnp.maximum(top, other)
    scales = [jnp.exp(one - top) for one in tops]
    total = totals[0] * scales[0]
    for one, scale in zip(totals[1:], scales[1:]):
        total = total + one * scale
    lane = lax.broadcasted_iota(jnp.int32, (row_count, 128), 1)
    first_half = lane < HD
    for pair in range(width // 128):
        cols = slice(pair * 128, (pair + 1) * 128)
        pick = lambda per_head: jnp.where(
            first_half, per_head[:, 2 * pair : 2 * pair + 1], per_head[:, 2 * pair + 1 : 2 * pair + 2]
        )
        acc = part_refs[0][:, cols].astype(jnp.float32) * pick(scales[0])
        for ref, scale in zip(part_refs[1:], scales[1:]):
            acc = acc + ref[:, cols].astype(jnp.float32) * pick(scale)
        out_ref[:, cols] = (acc / pick(total)).astype(out_ref.dtype)


def merge_partials(partials):
    row_count, padded = partials[0].shape
    width = padded - 128
    whole = lambda i: (0, 0)
    return pl.pallas_call(
        merge_kernel,
        grid=(1,),
        in_specs=[pl.BlockSpec(x.shape, whole) for x in partials],
        out_specs=pl.BlockSpec((row_count, width), whole),
        out_shape=jax.ShapeDtypeStruct((row_count, width), jnp.bfloat16),
    )(*partials)


def combine(current, incoming):
    out_a, top_a, total_a = current
    out_b, top_b, total_b = incoming
    new_top = jnp.maximum(top_a, top_b)
    scale_a = jnp.exp(top_a - new_top)
    scale_b = jnp.exp(top_b - new_top)
    return (
        out_a * scale_a[..., None] + out_b * scale_b[..., None],
        new_top,
        total_a * scale_a + total_b * scale_b,
    )


def window_visible(block_number, cache_len, row_count, block_rows):
    positions = block_number * block_rows + jnp.arange(block_rows, dtype=jnp.int32)
    query_pos = cache_len + jnp.arange(row_count, dtype=jnp.int32)
    return (positions[None, :] > query_pos[:, None] - WINDOW) & (positions[None, :] < cache_len)


def finish_heads(merged):
    summed, row_top, row_total = merged
    result = summed / row_total[..., None]
    head_count, row_count, head_size = result.shape
    return (
        jnp.transpose(result, (1, 0, 2))
        .reshape(row_count, head_count * head_size)
        .astype(jnp.bfloat16)
    )


def head_whole(projected):
    part = projected.astype(jnp.bfloat16)
    other = lax.ppermute(part, "head", [(0, 1), (1, 0)])
    return part.astype(jnp.float32) + other.astype(jnp.float32)


def full_norm(pre_norm, gain_vec, bias_vec):
    row_mean = jnp.mean(pre_norm, axis=-1, keepdims=True)
    centered = pre_norm - row_mean
    row_var = jnp.mean(centered * centered, axis=-1, keepdims=True)
    return centered * lax.rsqrt(row_var + norm_eps) * gain_vec + bias_vec


def project_back(rows_in, weight_t):
    return lax.dot_general(
        rows_in, weight_t, (((1,), (1,)), ((), ())), preferred_element_type=jnp.float32
    )


def per_device(
    queries,
    new_keys,
    new_values,
    sink_keys,
    sink_values,
    pool_keys,
    pool_values,
    block_ids,
    cache_lengths,
    cross_keys,
    cross_values,
    enc_lengths,
    hidden,
    w_out_t,
    gain_self,
    bias_self,
    w_cross_q,
    w_cross_out_t,
    gain_cross,
    bias_cross,
):
    device = lax.axis_index("blk")
    blk_count = lax.axis_size("blk")
    span_rows = queries.shape[0]
    slot_count = pool_keys.shape[1]
    block_rows = pool_keys.shape[2]
    sink_count = sink_keys.shape[1]
    own_length = lax.dynamic_index_in_dim(cache_lengths, device, keepdims=False)
    pad_rows = (-(sink_count + span_rows)) % 16
    pad_block = jnp.zeros((pad_rows, new_keys.shape[1]), new_keys.dtype)
    local_keys = jnp.concatenate([sink_keys[0], new_keys, pad_block], axis=0)
    local_values = jnp.concatenate([sink_values[0], new_values, pad_block], axis=0)
    local_bounds = jnp.array([sink_count, -FAR, sink_count + 1, FAR], jnp.int32)
    local_part = attention_partial(local_bounds, queries, local_keys, local_values, jnp.float32)
    partials = [local_part]
    for slot_step in range(1, slot_count + 1):
        travelling = passed_along(queries, "blk", slot_step)
        asker = (device - slot_step) % blk_count
        asker_length = lax.dynamic_index_in_dim(cache_lengths, asker, keepdims=False)
        held_block = lax.dynamic_index_in_dim(block_ids[:, slot_step - 1], device, keepdims=False)
        block_start = held_block * block_rows
        bounds = jnp.stack(
            [0, asker_length - WINDOW - block_start, FAR, asker_length - block_start]
        ).astype(jnp.int32)
        remote_part = attention_partial(
            bounds, travelling, pool_keys[0], pool_values[0], jnp.bfloat16, slot_step - 1,
            after=local_part if slot_step == 1 else None,
        )
        partials.append(passed_along(remote_part, "blk", -slot_step))
    attended = merge_partials(partials)
    self_proj = project_back(attended, w_out_t)
    head_index = lax.axis_index("head")
    head_width = hidden.shape[1]
    col_start = head_index * head_width
    own_cols = lax.dynamic_slice_in_dim(self_proj, col_start, head_width, 1) + hidden.astype(
        jnp.float32
    )
    with_residual = lax.dynamic_update_slice_in_dim(self_proj, own_cols, col_start, 1)
    pre_full = head_whole(with_residual)
    normed_full = full_norm(pre_full, gain_self, bias_self).astype(jnp.bfloat16)
    cross_query = jnp.dot(normed_full, w_cross_q, preferred_element_type=jnp.float32).astype(
        jnp.bfloat16
    )
    enc_bounds = jnp.stack([0, -FAR, FAR, enc_lengths[0]]).astype(jnp.int32)
    context = merge_partials(
        [attention_partial(enc_bounds, cross_query, cross_keys[0], cross_values[0], jnp.float32)]
    )
    cross_proj = project_back(context, w_cross_out_t)
    own_normed = lax.dynamic_slice_in_dim(normed_full, col_start, head_width, 1).astype(jnp.float32)
    own_cross = lax.dynamic_slice_in_dim(cross_proj, col_start, head_width, 1) + own_normed
    cross_residual = lax.dynamic_update_slice_in_dim(cross_proj, own_cross, col_start, 1)
    second_full = head_whole(cross_residual)
    full_out = full_norm(second_full, gain_cross, bias_cross).astype(jnp.bfloat16)
    layer_out = lax.dynamic_slice_in_dim(full_out, col_start, head_width, 1)
    return layer_out


def solution(mesh):
    placed = (
        P("blk", "head"),
        P("blk", "head"),
        P("blk", "head"),
        P("blk", None, "head"),
        P("blk", None, "head"),
        P("blk", None, None, "head"),
        P("blk", None, None, "head"),
        P(),
        P(),
        P("blk", None, "head"),
        P("blk", None, "head"),
        P("blk"),
        P("blk", "head"),
        P(None, "head"),
        P(),
        P(),
        P(None, "head"),
        P(None, "head"),
        P(),
        P(),
    )
    return jax.shard_map(
        per_device, mesh=mesh, in_specs=placed, out_specs=P("blk", "head"), check_vma=False
    )
```

```python
import functools

import jax
import jax.numpy as jnp
from jax import lax
from jax.experimental import pallas as pl
from jax.experimental.pallas import tpu as pltpu
from jax.sharding import PartitionSpec as P

HD = 64
WINDOW = 4096


masked_score = -1e30
top_floor = -1e20
FAR = 1 << 30
norm_eps = 1e-05


def passed_along(block, axis, distance):
    devices = range(lax.axis_size(axis))
    route = [((i - distance) % len(devices), i) for i in devices]
    return lax.ppermute(block, axis, route)


def partial_block(query_rows, key_rows, value_rows, visible):
    row_count = query_rows.shape[0]
    key_count = key_rows.shape[0]
    head_count = query_rows.shape[1] // HD
    query_heads = query_rows.reshape(row_count, head_count, HD)
    key_heads = key_rows.reshape(key_count, head_count, HD)
    value_heads = value_rows.reshape(key_count, head_count, HD)
    scores = jnp.einsum(
        "qhd,khd->hqk", query_heads, key_heads, preferred_element_type=jnp.float32
    ) * HD ** (-0.5)
    scores = scores + jnp.where(visible, 0.0, masked_score)[None]
    row_top = jnp.maximum(jnp.max(scores, axis=-1), top_floor)
    weights = jnp.exp(scores - row_top[..., None])
    row_total = jnp.sum(weights, axis=-1)
    summed = jnp.einsum(
        "hqk,khd->hqd",
        weights.astype(jnp.bfloat16),
        value_heads,
        preferred_element_type=jnp.float32,
    )
    return (summed, row_top, row_total)


def split_three(values):
    high = values.astype(jnp.bfloat16).astype(jnp.float32)
    rest = values - high
    middle = rest.astype(jnp.bfloat16).astype(jnp.float32)
    low = (rest - middle).astype(jnp.bfloat16).astype(jnp.float32)
    return (high, middle, low)


def window_kernel(offset, bounds_ref, q_ref, k_ref, v_ref, *rest):
    out_ref = rest[-1]
    row_count, width = q_ref.shape
    key_count = k_ref.shape[0]
    head_count = width // HD
    always = bounds_ref[offset]
    low = bounds_ref[offset + 1]
    upper = bounds_ref[offset + 2]
    high = bounds_ref[offset + 3]
    row = lax.broadcasted_iota(jnp.int32, (row_count, key_count), 0)
    col = lax.broadcasted_iota(jnp.int32, (row_count, key_count), 1)
    rel = col - row
    visible = (col < always) | ((rel > low) & (rel < upper) & (col < high))
    bias = jnp.where(visible, 0.0, masked_score)
    lane = lax.broadcasted_iota(jnp.int32, (row_count, 128), 1)
    first_half = lane < HD
    stats = jnp.zeros((row_count, 128), jnp.float32)
    for pair in range(width // 128):
        cols = slice(pair * 128, (pair + 1) * 128)
        q_pair = q_ref[:, cols]
        k_pair = k_ref[:, cols]
        v_pair = v_ref[:, cols]
        out_tile = jnp.zeros((row_count, 128), jnp.float32)
        for half in range(2):
            head = 2 * pair + half
            mine = first_half if half == 0 else jnp.logical_not(first_half)
            q_head = jnp.where(mine, q_pair, jnp.zeros_like(q_pair))
            scores = lax.dot_general(
                q_head, k_pair, (((1,), (1,)), ((), ())), preferred_element_type=jnp.float32
            ) * HD ** (-0.5) + bias
            top = jnp.maximum(jnp.max(scores, axis=1, keepdims=True), top_floor)
            weights = jnp.exp(scores - top)
            total = jnp.sum(weights, axis=1, keepdims=True)
            summed = jnp.dot(
                weights.astype(jnp.bfloat16), v_pair, preferred_element_type=jnp.float32
            )
            out_tile = jnp.where(mine, summed, out_tile)
            for piece, part in enumerate(split_three(top) + split_three(total)):
                stats = jnp.where(lane == piece * head_count + head, part, stats)
        out_ref[:, cols] = out_tile.astype(out_ref.dtype)
    out_ref[:, width : width + 128] = stats.astype(out_ref.dtype)


def attention_partial(bounds, query_rows, key_rows, value_rows, out_dtype, slot=None, after=None):
    row_count, width = query_rows.shape
    key_count = key_rows.shape[-2]
    whole = lambda i: (0, 0)
    if slot is None:
        key_spec = pl.BlockSpec((key_count, width), whole)
        offset = 0
    else:
        offset = 4 * slot
        key_spec = pl.BlockSpec((None, key_count, width), lambda i: (slot, 0, 0))
    operands = [bounds, query_rows, key_rows, value_rows]
    in_specs = [
        pl.BlockSpec(memory_space=pltpu.SMEM),
        pl.BlockSpec((row_count, width), whole),
        key_spec,
        key_spec,
    ]
    if after is not None:
        operands.append(after)
        in_specs.append(pl.BlockSpec(memory_space=pl.ANY))
    return pl.pallas_call(
        functools.partial(window_kernel, offset),
        grid=(1,),
        in_specs=in_specs,
        out_specs=pl.BlockSpec((row_count, width + 128), whole),
        out_shape=jax.ShapeDtypeStruct((row_count, width + 128), out_dtype),
    )(*operands)


def merge_kernel(*refs):
    part_refs = refs[:-1]
    out_ref = refs[-1]
    row_count, width = out_ref.shape
    head_count = width // HD
    tops = []
    totals = []
    for ref in part_refs:
        stats = ref[:, width : width + 128].astype(jnp.float32)
        piece = lambda k: stats[:, k * head_count : (k + 1) * head_count]
        tops.append(piece(0) + piece(1) + piece(2))
        totals.append(piece(3) + piece(4) + piece(5))
    top = tops[0]
    for other in tops[1:]:
        top = jnp.maximum(top, other)
    scales = [jnp.exp(one - top) for one in tops]
    total = totals[0] * scales[0]
    for one, scale in zip(totals[1:], scales[1:]):
        total = total + one * scale
    lane = lax.broadcasted_iota(jnp.int32, (row_count, 128), 1)
    first_half = lane < HD
    for pair in range(width // 128):
        cols = slice(pair * 128, (pair + 1) * 128)
        pick = lambda per_head: jnp.where(
            first_half, per_head[:, 2 * pair : 2 * pair + 1], per_head[:, 2 * pair + 1 : 2 * pair + 2]
        )
        acc = part_refs[0][:, cols].astype(jnp.float32) * pick(scales[0])
        for ref, scale in zip(part_refs[1:], scales[1:]):
            acc = acc + ref[:, cols].astype(jnp.float32) * pick(scale)
        out_ref[:, cols] = (acc / pick(total)).astype(out_ref.dtype)


def merge_partials(partials):
    row_count, padded = partials[0].shape
    width = padded - 128
    whole = lambda i: (0, 0)
    return pl.pallas_call(
        merge_kernel,
        grid=(1,),
        in_specs=[pl.BlockSpec(x.shape, whole) for x in partials],
        out_specs=pl.BlockSpec((row_count, width), whole),
        out_shape=jax.ShapeDtypeStruct((row_count, width), jnp.bfloat16),
    )(*partials)


def combine(current, incoming):
    out_a, top_a, total_a = current
    out_b, top_b, total_b = incoming
    new_top = jnp.maximum(top_a, top_b)
    scale_a = jnp.exp(top_a - new_top)
    scale_b = jnp.exp(top_b - new_top)
    return (
        out_a * scale_a[..., None] + out_b * scale_b[..., None],
        new_top,
        total_a * scale_a + total_b * scale_b,
    )


def window_visible(block_number, cache_len, row_count, block_rows):
    positions = block_number * block_rows + jnp.arange(block_rows, dtype=jnp.int32)
    query_pos = cache_len + jnp.arange(row_count, dtype=jnp.int32)
    return (positions[None, :] > query_pos[:, None] - WINDOW) & (positions[None, :] < cache_len)


def finish_heads(merged):
    summed, row_top, row_total = merged
    result = summed / row_total[..., None]
    head_count, row_count, head_size = result.shape
    return (
        jnp.transpose(result, (1, 0, 2))
        .reshape(row_count, head_count * head_size)
        .astype(jnp.bfloat16)
    )


def head_whole(projected):
    part = projected.astype(jnp.bfloat16)
    other = lax.ppermute(part, "head", [(0, 1), (1, 0)])
    return part.astype(jnp.float32) + other.astype(jnp.float32)


def full_norm(pre_norm, gain_vec, bias_vec):
    row_mean = jnp.mean(pre_norm, axis=-1, keepdims=True)
    centered = pre_norm - row_mean
    row_var = jnp.mean(centered * centered, axis=-1, keepdims=True)
    return centered * lax.rsqrt(row_var + norm_eps) * gain_vec + bias_vec


def project_back(rows_in, weight_t):
    return lax.dot_general(
        rows_in, weight_t, (((1,), (1,)), ((), ())), preferred_element_type=jnp.float32
    )


def per_device(
    queries,
    new_keys,
    new_values,
    sink_keys,
    sink_values,
    pool_keys,
    pool_values,
    block_ids,
    cache_lengths,
    cross_keys,
    cross_values,
    enc_lengths,
    hidden,
    w_out_t,
    gain_self,
    bias_self,
    w_cross_q,
    w_cross_out_t,
    gain_cross,
    bias_cross,
):
    device = lax.axis_index("blk")
    blk_count = lax.axis_size("blk")
    span_rows = queries.shape[0]
    slot_count = pool_keys.shape[1]
    block_rows = pool_keys.shape[2]
    sink_count = sink_keys.shape[1]
    own_length = lax.dynamic_index_in_dim(cache_lengths, device, keepdims=False)
    pad_rows = (-(sink_count + span_rows)) % 16
    pad_block = jnp.zeros((pad_rows, new_keys.shape[1]), new_keys.dtype)
    local_keys = jnp.concatenate([sink_keys[0], new_keys, pad_block], axis=0)
    local_values = jnp.concatenate([sink_values[0], new_values, pad_block], axis=0)
    local_bounds = jnp.array([sink_count, -FAR, sink_count + 1, FAR], jnp.int32)
    local_part = attention_partial(local_bounds, queries, local_keys, local_values, jnp.float32)
    slot_range = jnp.arange(slot_count, dtype=jnp.int32)
    asker_lengths = cache_lengths[(device - slot_range - 1) % blk_count]
    block_starts = lax.dynamic_index_in_dim(block_ids, device, keepdims=False) * block_rows
    bound_table = jnp.stack(
        [
            jnp.zeros_like(block_starts),
            asker_lengths - WINDOW - block_starts,
            jnp.full_like(block_starts, FAR),
            asker_lengths - block_starts,
        ],
        axis=1,
    ).reshape(-1)
    returned = {}
    for slot_step in range(1, slot_count + 1):
        travelling = passed_along(queries, "blk", slot_step)
        remote_part = attention_partial(
            bound_table, travelling, pool_keys[0], pool_values[0], jnp.bfloat16, slot_step - 1,
            after=local_part if slot_step == 1 else None,
        )
        returned[slot_step] = passed_along(remote_part, "blk", -slot_step)
    partials = [local_part] + [returned[step] for step in range(1, slot_count + 1)]
    attended = merge_partials(partials)
    self_proj = project_back(attended, w_out_t)
    head_index = lax.axis_index("head")
    head_width = hidden.shape[1]
    col_start = head_index * head_width
    own_cols = lax.dynamic_slice_in_dim(self_proj, col_start, head_width, 1) + hidden.astype(
        jnp.float32
    )
    with_residual = lax.dynamic_update_slice_in_dim(self_proj, own_cols, col_start, 1)
    pre_full = head_whole(with_residual)
    normed_full = full_norm(pre_full, gain_self, bias_self).astype(jnp.bfloat16)
    cross_query = jnp.dot(normed_full, w_cross_q, preferred_element_type=jnp.float32).astype(
        jnp.bfloat16
    )
    enc_bounds = jnp.stack([0, -FAR, FAR, enc_lengths[0]]).astype(jnp.int32)
    context = merge_partials(
        [attention_partial(enc_bounds, cross_query, cross_keys[0], cross_values[0], jnp.float32)]
    )
    cross_proj = project_back(context, w_cross_out_t)
    own_normed = lax.dynamic_slice_in_dim(normed_full, col_start, head_width, 1).astype(jnp.float32)
    own_cross = lax.dynamic_slice_in_dim(cross_proj, col_start, head_width, 1) + own_normed
    cross_residual = lax.dynamic_update_slice_in_dim(cross_proj, own_cross, col_start, 1)
    second_full = head_whole(cross_residual)
    full_out = full_norm(second_full, gain_cross, bias_cross).astype(jnp.bfloat16)
    layer_out = lax.dynamic_slice_in_dim(full_out, col_start, head_width, 1)
    return layer_out


def solution(mesh):
    placed = (
        P("blk", "head"),
        P("blk", "head"),
        P("blk", "head"),
        P("blk", None, "head"),
        P("blk", None, "head"),
        P("blk", None, None, "head"),
        P("blk", None, None, "head"),
        P(),
        P(),
        P("blk", None, "head"),
        P("blk", None, "head"),
        P("blk"),
        P("blk", "head"),
        P(None, "head"),
        P(),
        P(),
        P(None, "head"),
        P(None, "head"),
        P(),
        P(),
    )
    return jax.shard_map(
        per_device, mesh=mesh, in_specs=placed, out_specs=P("blk", "head"), check_vma=False
    )
```

```python
import functools

import jax
import jax.numpy as jnp
from jax import lax
from jax.experimental import pallas as pl
from jax.experimental.pallas import tpu as pltpu
from jax.sharding import PartitionSpec as P

HD = 64
WINDOW = 4096


masked_score = -1e30
top_floor = -1e20
FAR = 1 << 30
RELAY_SPAN = 4
norm_eps = 1e-05


def passed_along(block, axis, distance):
    devices = range(lax.axis_size(axis))
    route = [((i - distance) % len(devices), i) for i in devices]
    return lax.ppermute(block, axis, route)


def partial_block(query_rows, key_rows, value_rows, visible):
    row_count = query_rows.shape[0]
    key_count = key_rows.shape[0]
    head_count = query_rows.shape[1] // HD
    query_heads = query_rows.reshape(row_count, head_count, HD)
    key_heads = key_rows.reshape(key_count, head_count, HD)
    value_heads = value_rows.reshape(key_count, head_count, HD)
    scores = jnp.einsum(
        "qhd,khd->hqk", query_heads, key_heads, preferred_element_type=jnp.float32
    ) * HD ** (-0.5)
    scores = scores + jnp.where(visible, 0.0, masked_score)[None]
    row_top = jnp.maximum(jnp.max(scores, axis=-1), top_floor)
    weights = jnp.exp(scores - row_top[..., None])
    row_total = jnp.sum(weights, axis=-1)
    summed = jnp.einsum(
        "hqk,khd->hqd",
        weights.astype(jnp.bfloat16),
        value_heads,
        preferred_element_type=jnp.float32,
    )
    return (summed, row_top, row_total)


def split_three(values):
    high = values.astype(jnp.bfloat16).astype(jnp.float32)
    rest = values - high
    middle = rest.astype(jnp.bfloat16).astype(jnp.float32)
    low = (rest - middle).astype(jnp.bfloat16).astype(jnp.float32)
    return (high, middle, low)


def window_kernel(offset, bounds_ref, q_ref, k_ref, v_ref, *rest):
    out_ref = rest[-1]
    row_count, width = q_ref.shape
    key_count = k_ref.shape[0]
    head_count = width // HD
    always = bounds_ref[offset]
    low = bounds_ref[offset + 1]
    upper = bounds_ref[offset + 2]
    high = bounds_ref[offset + 3]
    row = lax.broadcasted_iota(jnp.int32, (row_count, key_count), 0)
    col = lax.broadcasted_iota(jnp.int32, (row_count, key_count), 1)
    rel = col - row
    visible = (col < always) | ((rel > low) & (rel < upper) & (col < high))
    bias = jnp.where(visible, 0.0, masked_score)
    lane = lax.broadcasted_iota(jnp.int32, (row_count, 128), 1)
    first_half = lane < HD
    stats = jnp.zeros((row_count, 128), jnp.float32)
    for pair in range(width // 128):
        cols = slice(pair * 128, (pair + 1) * 128)
        q_pair = q_ref[:, cols]
        k_pair = k_ref[:, cols]
        v_pair = v_ref[:, cols]
        out_tile = jnp.zeros((row_count, 128), jnp.float32)
        for half in range(2):
            head = 2 * pair + half
            mine = first_half if half == 0 else jnp.logical_not(first_half)
            q_head = jnp.where(mine, q_pair, jnp.zeros_like(q_pair))
            scores = lax.dot_general(
                q_head, k_pair, (((1,), (1,)), ((), ())), preferred_element_type=jnp.float32
            ) * HD ** (-0.5) + bias
            top = jnp.maximum(jnp.max(scores, axis=1, keepdims=True), top_floor)
            weights = jnp.exp(scores - top)
            total = jnp.sum(weights, axis=1, keepdims=True)
            summed = jnp.dot(
                weights.astype(jnp.bfloat16), v_pair, preferred_element_type=jnp.float32
            )
            out_tile = jnp.where(mine, summed, out_tile)
            for piece, part in enumerate(split_three(top) + split_three(total)):
                stats = jnp.where(lane == piece * head_count + head, part, stats)
        out_ref[:, cols] = out_tile.astype(out_ref.dtype)
    out_ref[:, width : width + 128] = stats.astype(out_ref.dtype)


def attention_partial(bounds, query_rows, key_rows, value_rows, out_dtype, slot=None, after=None):
    row_count, width = query_rows.shape
    key_count = key_rows.shape[-2]
    whole = lambda i: (0, 0)
    if slot is None:
        key_spec = pl.BlockSpec((key_count, width), whole)
        offset = 0
    else:
        offset = 4 * slot
        key_spec = pl.BlockSpec((None, key_count, width), lambda i: (slot, 0, 0))
    operands = [bounds, query_rows, key_rows, value_rows]
    in_specs = [
        pl.BlockSpec(memory_space=pltpu.SMEM),
        pl.BlockSpec((row_count, width), whole),
        key_spec,
        key_spec,
    ]
    if after is not None:
        operands.append(after)
        in_specs.append(pl.BlockSpec(memory_space=pl.ANY))
    return pl.pallas_call(
        functools.partial(window_kernel, offset),
        grid=(1,),
        in_specs=in_specs,
        out_specs=pl.BlockSpec((row_count, width + 128), whole),
        out_shape=jax.ShapeDtypeStruct((row_count, width + 128), out_dtype),
    )(*operands)


def merge_kernel(*refs):
    part_refs = refs[:-1]
    out_ref = refs[-1]
    row_count, width = out_ref.shape
    head_count = width // HD
    tops = []
    totals = []
    for ref in part_refs:
        stats = ref[:, width : width + 128].astype(jnp.float32)
        piece = lambda k: stats[:, k * head_count : (k + 1) * head_count]
        tops.append(piece(0) + piece(1) + piece(2))
        totals.append(piece(3) + piece(4) + piece(5))
    top = tops[0]
    for other in tops[1:]:
        top = jnp.maximum(top, other)
    scales = [jnp.exp(one - top) for one in tops]
    total = totals[0] * scales[0]
    for one, scale in zip(totals[1:], scales[1:]):
        total = total + one * scale
    lane = lax.broadcasted_iota(jnp.int32, (row_count, 128), 1)
    first_half = lane < HD
    for pair in range(width // 128):
        cols = slice(pair * 128, (pair + 1) * 128)
        pick = lambda per_head: jnp.where(
            first_half, per_head[:, 2 * pair : 2 * pair + 1], per_head[:, 2 * pair + 1 : 2 * pair + 2]
        )
        acc = part_refs[0][:, cols].astype(jnp.float32) * pick(scales[0])
        for ref, scale in zip(part_refs[1:], scales[1:]):
            acc = acc + ref[:, cols].astype(jnp.float32) * pick(scale)
        out_ref[:, cols] = (acc / pick(total)).astype(out_ref.dtype)


def merge_partials(partials):
    row_count, padded = partials[0].shape
    width = padded - 128
    whole = lambda i: (0, 0)
    return pl.pallas_call(
        merge_kernel,
        grid=(1,),
        in_specs=[pl.BlockSpec(x.shape, whole) for x in partials],
        out_specs=pl.BlockSpec((row_count, width), whole),
        out_shape=jax.ShapeDtypeStruct((row_count, width), jnp.bfloat16),
    )(*partials)


def combine(current, incoming):
    out_a, top_a, total_a = current
    out_b, top_b, total_b = incoming
    new_top = jnp.maximum(top_a, top_b)
    scale_a = jnp.exp(top_a - new_top)
    scale_b = jnp.exp(top_b - new_top)
    return (
        out_a * scale_a[..., None] + out_b * scale_b[..., None],
        new_top,
        total_a * scale_a + total_b * scale_b,
    )


def window_visible(block_number, cache_len, row_count, block_rows):
    positions = block_number * block_rows + jnp.arange(block_rows, dtype=jnp.int32)
    query_pos = cache_len + jnp.arange(row_count, dtype=jnp.int32)
    return (positions[None, :] > query_pos[:, None] - WINDOW) & (positions[None, :] < cache_len)


def finish_heads(merged):
    summed, row_top, row_total = merged
    result = summed / row_total[..., None]
    head_count, row_count, head_size = result.shape
    return (
        jnp.transpose(result, (1, 0, 2))
        .reshape(row_count, head_count * head_size)
        .astype(jnp.bfloat16)
    )


def head_whole(projected):
    part = projected.astype(jnp.bfloat16)
    other = lax.ppermute(part, "head", [(0, 1), (1, 0)])
    return part.astype(jnp.float32) + other.astype(jnp.float32)


def full_norm(pre_norm, gain_vec, bias_vec):
    row_mean = jnp.mean(pre_norm, axis=-1, keepdims=True)
    centered = pre_norm - row_mean
    row_var = jnp.mean(centered * centered, axis=-1, keepdims=True)
    return centered * lax.rsqrt(row_var + norm_eps) * gain_vec + bias_vec


def project_back(rows_in, weight_t):
    return lax.dot_general(
        rows_in, weight_t, (((1,), (1,)), ((), ())), preferred_element_type=jnp.float32
    )


def per_device(
    queries,
    new_keys,
    new_values,
    sink_keys,
    sink_values,
    pool_keys,
    pool_values,
    block_ids,
    cache_lengths,
    cross_keys,
    cross_values,
    enc_lengths,
    hidden,
    w_out_t,
    gain_self,
    bias_self,
    w_cross_q,
    w_cross_out_t,
    gain_cross,
    bias_cross,
):
    device = lax.axis_index("blk")
    blk_count = lax.axis_size("blk")
    span_rows = queries.shape[0]
    slot_count = pool_keys.shape[1]
    block_rows = pool_keys.shape[2]
    sink_count = sink_keys.shape[1]
    own_length = lax.dynamic_index_in_dim(cache_lengths, device, keepdims=False)
    pad_rows = (-(sink_count + span_rows)) % 16
    pad_block = jnp.zeros((pad_rows, new_keys.shape[1]), new_keys.dtype)
    local_keys = jnp.concatenate([sink_keys[0], new_keys, pad_block], axis=0)
    local_values = jnp.concatenate([sink_values[0], new_values, pad_block], axis=0)
    local_bounds = jnp.array([sink_count, -FAR, sink_count + 1, FAR], jnp.int32)
    local_part = attention_partial(local_bounds, queries, local_keys, local_values, jnp.float32)
    slot_range = jnp.arange(slot_count, dtype=jnp.int32)
    asker_lengths = cache_lengths[(device - slot_range - 1) % blk_count]
    block_starts = lax.dynamic_index_in_dim(block_ids, device, keepdims=False) * block_rows
    bound_table = jnp.stack(
        [
            jnp.zeros_like(block_starts),
            asker_lengths - WINDOW - block_starts,
            jnp.full_like(block_starts, FAR),
            asker_lengths - block_starts,
        ],
        axis=1,
    ).reshape(-1)
    returned = {}
    held_queries = {}
    for slot_step in range(1, slot_count + 1):
        if slot_step % RELAY_SPAN in (0, 1) and slot_step < 2 * RELAY_SPAN + 1:
            travelling = passed_along(queries, "blk", slot_step)
        else:
            travelling = passed_along(held_queries[slot_step - 1], "blk", 1)
        remote_part = attention_partial(
            bound_table, travelling, pool_keys[0], pool_values[0], jnp.bfloat16, slot_step - 1,
            after=local_part if slot_step == 1 else None,
        )
        held_queries[slot_step], remote_part = lax.optimization_barrier((travelling, remote_part))
        returned[slot_step] = passed_along(remote_part, "blk", -slot_step)
    partials = [local_part] + [returned[step] for step in range(1, slot_count + 1)]
    attended = merge_partials(partials)
    self_proj = project_back(attended, w_out_t)
    head_index = lax.axis_index("head")
    head_width = hidden.shape[1]
    col_start = head_index * head_width
    own_cols = lax.dynamic_slice_in_dim(self_proj, col_start, head_width, 1) + hidden.astype(
        jnp.float32
    )
    with_residual = lax.dynamic_update_slice_in_dim(self_proj, own_cols, col_start, 1)
    pre_full = head_whole(with_residual)
    normed_full = full_norm(pre_full, gain_self, bias_self).astype(jnp.bfloat16)
    cross_query = jnp.dot(normed_full, w_cross_q, preferred_element_type=jnp.float32).astype(
        jnp.bfloat16
    )
    enc_bounds = jnp.stack([0, -FAR, FAR, enc_lengths[0]]).astype(jnp.int32)
    context = merge_partials(
        [attention_partial(enc_bounds, cross_query, cross_keys[0], cross_values[0], jnp.float32)]
    )
    cross_proj = project_back(context, w_cross_out_t)
    own_normed = lax.dynamic_slice_in_dim(normed_full, col_start, head_width, 1).astype(jnp.float32)
    own_cross = lax.dynamic_slice_in_dim(cross_proj, col_start, head_width, 1) + own_normed
    cross_residual = lax.dynamic_update_slice_in_dim(cross_proj, own_cross, col_start, 1)
    second_full = head_whole(cross_residual)
    full_out = full_norm(second_full, gain_cross, bias_cross).astype(jnp.bfloat16)
    layer_out = lax.dynamic_slice_in_dim(full_out, col_start, head_width, 1)
    return layer_out


def solution(mesh):
    placed = (
        P("blk", "head"),
        P("blk", "head"),
        P("blk", "head"),
        P("blk", None, "head"),
        P("blk", None, "head"),
        P("blk", None, None, "head"),
        P("blk", None, None, "head"),
        P(),
        P(),
        P("blk", None, "head"),
        P("blk", None, "head"),
        P("blk"),
        P("blk", "head"),
        P(None, "head"),
        P(),
        P(),
        P(None, "head"),
        P(None, "head"),
        P(),
        P(),
    )
    return jax.shard_map(
        per_device, mesh=mesh, in_specs=placed, out_specs=P("blk", "head"), check_vma=False
    )
```

```python
import functools

import jax
import jax.numpy as jnp
from jax import lax
from jax.experimental import pallas as pl
from jax.experimental.pallas import tpu as pltpu
from jax.sharding import PartitionSpec as P

HD = 64
WINDOW = 4096


masked_score = -1e30
top_floor = -1e20
FAR = 1 << 30
SEND_CHAINS = ((1, 2, 3, 7, 6), (4, 8, 5, 9))
norm_eps = 1e-05


def passed_along(block, axis, distance):
    devices = range(lax.axis_size(axis))
    route = [((i - distance) % len(devices), i) for i in devices]
    return lax.ppermute(block, axis, route)


def partial_block(query_rows, key_rows, value_rows, visible):
    row_count = query_rows.shape[0]
    key_count = key_rows.shape[0]
    head_count = query_rows.shape[1] // HD
    query_heads = query_rows.reshape(row_count, head_count, HD)
    key_heads = key_rows.reshape(key_count, head_count, HD)
    value_heads = value_rows.reshape(key_count, head_count, HD)
    scores = jnp.einsum(
        "qhd,khd->hqk", query_heads, key_heads, preferred_element_type=jnp.float32
    ) * HD ** (-0.5)
    scores = scores + jnp.where(visible, 0.0, masked_score)[None]
    row_top = jnp.maximum(jnp.max(scores, axis=-1), top_floor)
    weights = jnp.exp(scores - row_top[..., None])
    row_total = jnp.sum(weights, axis=-1)
    summed = jnp.einsum(
        "hqk,khd->hqd",
        weights.astype(jnp.bfloat16),
        value_heads,
        preferred_element_type=jnp.float32,
    )
    return (summed, row_top, row_total)


def split_three(values):
    high = values.astype(jnp.bfloat16).astype(jnp.float32)
    rest = values - high
    middle = rest.astype(jnp.bfloat16).astype(jnp.float32)
    low = (rest - middle).astype(jnp.bfloat16).astype(jnp.float32)
    return (high, middle, low)


def window_kernel(offset, bounds_ref, q_ref, k_ref, v_ref, *rest):
    out_ref = rest[-1]
    row_count, width = q_ref.shape
    key_count = k_ref.shape[0]
    head_count = width // HD
    always = bounds_ref[offset]
    low = bounds_ref[offset + 1]
    upper = bounds_ref[offset + 2]
    high = bounds_ref[offset + 3]
    row = lax.broadcasted_iota(jnp.int32, (row_count, key_count), 0)
    col = lax.broadcasted_iota(jnp.int32, (row_count, key_count), 1)
    rel = col - row
    visible = (col < always) | ((rel > low) & (rel < upper) & (col < high))
    bias = jnp.where(visible, 0.0, masked_score)
    lane = lax.broadcasted_iota(jnp.int32, (row_count, 128), 1)
    first_half = lane < HD
    stats = jnp.zeros((row_count, 128), jnp.float32)
    for pair in range(width // 128):
        cols = slice(pair * 128, (pair + 1) * 128)
        q_pair = q_ref[:, cols]
        k_pair = k_ref[:, cols]
        v_pair = v_ref[:, cols]
        out_tile = jnp.zeros((row_count, 128), jnp.float32)
        for half in range(2):
            head = 2 * pair + half
            mine = first_half if half == 0 else jnp.logical_not(first_half)
            q_head = jnp.where(mine, q_pair, jnp.zeros_like(q_pair))
            scores = lax.dot_general(
                q_head, k_pair, (((1,), (1,)), ((), ())), preferred_element_type=jnp.float32
            ) * HD ** (-0.5) + bias
            top = jnp.maximum(jnp.max(scores, axis=1, keepdims=True), top_floor)
            weights = jnp.exp(scores - top)
            total = jnp.sum(weights, axis=1, keepdims=True)
            summed = jnp.dot(
                weights.astype(jnp.bfloat16), v_pair, preferred_element_type=jnp.float32
            )
            out_tile = jnp.where(mine, summed, out_tile)
            for piece, part in enumerate(split_three(top) + split_three(total)):
                stats = jnp.where(lane == piece * head_count + head, part, stats)
        out_ref[:, cols] = out_tile.astype(out_ref.dtype)
    out_ref[:, width : width + 128] = stats.astype(out_ref.dtype)


def attention_partial(bounds, query_rows, key_rows, value_rows, out_dtype, slot=None, after=None):
    row_count, width = query_rows.shape
    key_count = key_rows.shape[-2]
    whole = lambda i: (0, 0)
    if slot is None:
        key_spec = pl.BlockSpec((key_count, width), whole)
        offset = 0
    else:
        offset = 4 * slot
        key_spec = pl.BlockSpec((None, key_count, width), lambda i: (slot, 0, 0))
    operands = [bounds, query_rows, key_rows, value_rows]
    in_specs = [
        pl.BlockSpec(memory_space=pltpu.SMEM),
        pl.BlockSpec((row_count, width), whole),
        key_spec,
        key_spec,
    ]
    if after is not None:
        operands.append(after)
        in_specs.append(pl.BlockSpec(memory_space=pl.ANY))
    return pl.pallas_call(
        functools.partial(window_kernel, offset),
        grid=(1,),
        in_specs=in_specs,
        out_specs=pl.BlockSpec((row_count, width + 128), whole),
        out_shape=jax.ShapeDtypeStruct((row_count, width + 128), out_dtype),
    )(*operands)


def merge_kernel(*refs):
    part_refs = refs[:-1]
    out_ref = refs[-1]
    row_count, width = out_ref.shape
    head_count = width // HD
    tops = []
    totals = []
    for ref in part_refs:
        stats = ref[:, width : width + 128].astype(jnp.float32)
        piece = lambda k: stats[:, k * head_count : (k + 1) * head_count]
        tops.append(piece(0) + piece(1) + piece(2))
        totals.append(piece(3) + piece(4) + piece(5))
    top = tops[0]
    for other in tops[1:]:
        top = jnp.maximum(top, other)
    scales = [jnp.exp(one - top) for one in tops]
    total = totals[0] * scales[0]
    for one, scale in zip(totals[1:], scales[1:]):
        total = total + one * scale
    lane = lax.broadcasted_iota(jnp.int32, (row_count, 128), 1)
    first_half = lane < HD
    for pair in range(width // 128):
        cols = slice(pair * 128, (pair + 1) * 128)
        pick = lambda per_head: jnp.where(
            first_half, per_head[:, 2 * pair : 2 * pair + 1], per_head[:, 2 * pair + 1 : 2 * pair + 2]
        )
        acc = part_refs[0][:, cols].astype(jnp.float32) * pick(scales[0])
        for ref, scale in zip(part_refs[1:], scales[1:]):
            acc = acc + ref[:, cols].astype(jnp.float32) * pick(scale)
        out_ref[:, cols] = (acc / pick(total)).astype(out_ref.dtype)


def merge_partials(partials):
    row_count, padded = partials[0].shape
    width = padded - 128
    whole = lambda i: (0, 0)
    return pl.pallas_call(
        merge_kernel,
        grid=(1,),
        in_specs=[pl.BlockSpec(x.shape, whole) for x in partials],
        out_specs=pl.BlockSpec((row_count, width), whole),
        out_shape=jax.ShapeDtypeStruct((row_count, width), jnp.bfloat16),
    )(*partials)


def combine(current, incoming):
    out_a, top_a, total_a = current
    out_b, top_b, total_b = incoming
    new_top = jnp.maximum(top_a, top_b)
    scale_a = jnp.exp(top_a - new_top)
    scale_b = jnp.exp(top_b - new_top)
    return (
        out_a * scale_a[..., None] + out_b * scale_b[..., None],
        new_top,
        total_a * scale_a + total_b * scale_b,
    )


def window_visible(block_number, cache_len, row_count, block_rows):
    positions = block_number * block_rows + jnp.arange(block_rows, dtype=jnp.int32)
    query_pos = cache_len + jnp.arange(row_count, dtype=jnp.int32)
    return (positions[None, :] > query_pos[:, None] - WINDOW) & (positions[None, :] < cache_len)


def finish_heads(merged):
    summed, row_top, row_total = merged
    result = summed / row_total[..., None]
    head_count, row_count, head_size = result.shape
    return (
        jnp.transpose(result, (1, 0, 2))
        .reshape(row_count, head_count * head_size)
        .astype(jnp.bfloat16)
    )


def head_whole(projected):
    part = projected.astype(jnp.bfloat16)
    other = lax.ppermute(part, "head", [(0, 1), (1, 0)])
    return part.astype(jnp.float32) + other.astype(jnp.float32)


def full_norm(pre_norm, gain_vec, bias_vec):
    row_mean = jnp.mean(pre_norm, axis=-1, keepdims=True)
    centered = pre_norm - row_mean
    row_var = jnp.mean(centered * centered, axis=-1, keepdims=True)
    return centered * lax.rsqrt(row_var + norm_eps) * gain_vec + bias_vec


def project_back(rows_in, weight_t):
    return lax.dot_general(
        rows_in, weight_t, (((1,), (1,)), ((), ())), preferred_element_type=jnp.float32
    )


def per_device(
    queries,
    new_keys,
    new_values,
    sink_keys,
    sink_values,
    pool_keys,
    pool_values,
    block_ids,
    cache_lengths,
    cross_keys,
    cross_values,
    enc_lengths,
    hidden,
    w_out_t,
    gain_self,
    bias_self,
    w_cross_q,
    w_cross_out_t,
    gain_cross,
    bias_cross,
):
    device = lax.axis_index("blk")
    blk_count = lax.axis_size("blk")
    span_rows = queries.shape[0]
    slot_count = pool_keys.shape[1]
    block_rows = pool_keys.shape[2]
    sink_count = sink_keys.shape[1]
    own_length = lax.dynamic_index_in_dim(cache_lengths, device, keepdims=False)
    pad_rows = (-(sink_count + span_rows)) % 16
    pad_block = jnp.zeros((pad_rows, new_keys.shape[1]), new_keys.dtype)
    local_keys = jnp.concatenate([sink_keys[0], new_keys, pad_block], axis=0)
    local_values = jnp.concatenate([sink_values[0], new_values, pad_block], axis=0)
    local_bounds = jnp.array([sink_count, -FAR, sink_count + 1, FAR], jnp.int32)
    local_part = attention_partial(local_bounds, queries, local_keys, local_values, jnp.float32)
    slot_range = jnp.arange(slot_count, dtype=jnp.int32)
    asker_lengths = cache_lengths[(device - slot_range - 1) % blk_count]
    block_starts = lax.dynamic_index_in_dim(block_ids, device, keepdims=False) * block_rows
    bound_table = jnp.stack(
        [
            jnp.zeros_like(block_starts),
            asker_lengths - WINDOW - block_starts,
            jnp.full_like(block_starts, FAR),
            asker_lengths - block_starts,
        ],
        axis=1,
    ).reshape(-1)
    returned = {}
    chains = [chain for chain in SEND_CHAINS if max(chain) <= slot_count]
    if sorted(sum(chains, ())) != list(range(1, slot_count + 1)):
        chains = [tuple(range(1, slot_count + 1))]
    for chain in chains:
        previous = None
        for slot_step in chain:
            outgoing = queries
            if previous is not None:
                outgoing, _ = lax.optimization_barrier((queries, previous))
            remote_part = attention_partial(
                bound_table, passed_along(outgoing, "blk", slot_step), pool_keys[0],
                pool_values[0], jnp.bfloat16, slot_step - 1,
                after=local_part if previous is None else None,
            )
            returned[slot_step] = passed_along(remote_part, "blk", -slot_step)
            previous = remote_part
    partials = [local_part] + [returned[step] for step in range(1, slot_count + 1)]
    attended = merge_partials(partials)
    self_proj = project_back(attended, w_out_t)
    head_index = lax.axis_index("head")
    head_width = hidden.shape[1]
    col_start = head_index * head_width
    own_cols = lax.dynamic_slice_in_dim(self_proj, col_start, head_width, 1) + hidden.astype(
        jnp.float32
    )
    with_residual = lax.dynamic_update_slice_in_dim(self_proj, own_cols, col_start, 1)
    pre_full = head_whole(with_residual)
    normed_full = full_norm(pre_full, gain_self, bias_self).astype(jnp.bfloat16)
    cross_query = jnp.dot(normed_full, w_cross_q, preferred_element_type=jnp.float32).astype(
        jnp.bfloat16
    )
    enc_bounds = jnp.stack([0, -FAR, FAR, enc_lengths[0]]).astype(jnp.int32)
    context = merge_partials(
        [attention_partial(enc_bounds, cross_query, cross_keys[0], cross_values[0], jnp.float32)]
    )
    cross_proj = project_back(context, w_cross_out_t)
    own_normed = lax.dynamic_slice_in_dim(normed_full, col_start, head_width, 1).astype(jnp.float32)
    own_cross = lax.dynamic_slice_in_dim(cross_proj, col_start, head_width, 1) + own_normed
    cross_residual = lax.dynamic_update_slice_in_dim(cross_proj, own_cross, col_start, 1)
    second_full = head_whole(cross_residual)
    full_out = full_norm(second_full, gain_cross, bias_cross).astype(jnp.bfloat16)
    layer_out = lax.dynamic_slice_in_dim(full_out, col_start, head_width, 1)
    return layer_out


def solution(mesh):
    placed = (
        P("blk", "head"),
        P("blk", "head"),
        P("blk", "head"),
        P("blk", None, "head"),
        P("blk", None, "head"),
        P("blk", None, None, "head"),
        P("blk", None, None, "head"),
        P(),
        P(),
        P("blk", None, "head"),
        P("blk", None, "head"),
        P("blk"),
        P("blk", "head"),
        P(None, "head"),
        P(),
        P(),
        P(None, "head"),
        P(None, "head"),
        P(),
        P(),
    )
    return jax.shard_map(
        per_device, mesh=mesh, in_specs=placed, out_specs=P("blk", "head"), check_vma=False
    )
```

```python
import functools

import jax
import jax.numpy as jnp
from jax import lax
from jax.experimental import pallas as pl
from jax.experimental.pallas import tpu as pltpu
from jax.sharding import PartitionSpec as P

HD = 64
WINDOW = 4096


masked_score = -1e30
top_floor = -1e20
FAR = 1 << 30
EARLY_SLOTS = (1, 6, 7, 8)
norm_eps = 1e-05


def passed_along(block, axis, distance):
    devices = range(lax.axis_size(axis))
    route = [((i - distance) % len(devices), i) for i in devices]
    return lax.ppermute(block, axis, route)


def partial_block(query_rows, key_rows, value_rows, visible):
    row_count = query_rows.shape[0]
    key_count = key_rows.shape[0]
    head_count = query_rows.shape[1] // HD
    query_heads = query_rows.reshape(row_count, head_count, HD)
    key_heads = key_rows.reshape(key_count, head_count, HD)
    value_heads = value_rows.reshape(key_count, head_count, HD)
    scores = jnp.einsum(
        "qhd,khd->hqk", query_heads, key_heads, preferred_element_type=jnp.float32
    ) * HD ** (-0.5)
    scores = scores + jnp.where(visible, 0.0, masked_score)[None]
    row_top = jnp.maximum(jnp.max(scores, axis=-1), top_floor)
    weights = jnp.exp(scores - row_top[..., None])
    row_total = jnp.sum(weights, axis=-1)
    summed = jnp.einsum(
        "hqk,khd->hqd",
        weights.astype(jnp.bfloat16),
        value_heads,
        preferred_element_type=jnp.float32,
    )
    return (summed, row_top, row_total)


def split_three(values):
    high = values.astype(jnp.bfloat16).astype(jnp.float32)
    rest = values - high
    middle = rest.astype(jnp.bfloat16).astype(jnp.float32)
    low = (rest - middle).astype(jnp.bfloat16).astype(jnp.float32)
    return (high, middle, low)


def window_kernel(offset, bounds_ref, q_ref, k_ref, v_ref, *rest):
    out_ref = rest[-1]
    row_count, width = q_ref.shape
    key_count = k_ref.shape[0]
    head_count = width // HD
    always = bounds_ref[offset]
    low = bounds_ref[offset + 1]
    upper = bounds_ref[offset + 2]
    high = bounds_ref[offset + 3]
    row = lax.broadcasted_iota(jnp.int32, (row_count, key_count), 0)
    col = lax.broadcasted_iota(jnp.int32, (row_count, key_count), 1)
    rel = col - row
    visible = (col < always) | ((rel > low) & (rel < upper) & (col < high))
    bias = jnp.where(visible, 0.0, masked_score)
    lane = lax.broadcasted_iota(jnp.int32, (row_count, 128), 1)
    first_half = lane < HD
    stats = jnp.zeros((row_count, 128), jnp.float32)
    for pair in range(width // 128):
        cols = slice(pair * 128, (pair + 1) * 128)
        q_pair = q_ref[:, cols]
        k_pair = k_ref[:, cols]
        v_pair = v_ref[:, cols]
        out_tile = jnp.zeros((row_count, 128), jnp.float32)
        for half in range(2):
            head = 2 * pair + half
            mine = first_half if half == 0 else jnp.logical_not(first_half)
            q_head = jnp.where(mine, q_pair, jnp.zeros_like(q_pair))
            scores = lax.dot_general(
                q_head, k_pair, (((1,), (1,)), ((), ())), preferred_element_type=jnp.float32
            ) * HD ** (-0.5) + bias
            top = jnp.maximum(jnp.max(scores, axis=1, keepdims=True), top_floor)
            weights = jnp.exp(scores - top)
            total = jnp.sum(weights, axis=1, keepdims=True)
            summed = jnp.dot(
                weights.astype(jnp.bfloat16), v_pair, preferred_element_type=jnp.float32
            )
            out_tile = jnp.where(mine, summed, out_tile)
            for piece, part in enumerate(split_three(top) + split_three(total)):
                stats = jnp.where(lane == piece * head_count + head, part, stats)
        out_ref[:, cols] = out_tile.astype(out_ref.dtype)
    out_ref[:, width : width + 128] = stats.astype(out_ref.dtype)


def attention_partial(bounds, query_rows, key_rows, value_rows, out_dtype, slot=None, after=None):
    row_count, width = query_rows.shape
    key_count = key_rows.shape[-2]
    whole = lambda i: (0, 0)
    if slot is None:
        key_spec = pl.BlockSpec((key_count, width), whole)
        offset = 0
    else:
        offset = 4 * slot
        key_spec = pl.BlockSpec((None, key_count, width), lambda i: (slot, 0, 0))
    operands = [bounds, query_rows, key_rows, value_rows]
    in_specs = [
        pl.BlockSpec(memory_space=pltpu.SMEM),
        pl.BlockSpec((row_count, width), whole),
        key_spec,
        key_spec,
    ]
    if after is not None:
        operands.append(after)
        in_specs.append(pl.BlockSpec(memory_space=pl.ANY))
    return pl.pallas_call(
        functools.partial(window_kernel, offset),
        grid=(1,),
        in_specs=in_specs,
        out_specs=pl.BlockSpec((row_count, width + 128), whole),
        out_shape=jax.ShapeDtypeStruct((row_count, width + 128), out_dtype),
    )(*operands)


def merge_kernel(finish, *refs):
    part_refs = refs[:-1]
    out_ref = refs[-1]
    row_count = out_ref.shape[0]
    width = part_refs[0].shape[1] - 128
    head_count = width // HD
    tops = []
    totals = []
    for ref in part_refs:
        stats = ref[:, width : width + 128].astype(jnp.float32)
        piece = lambda k: stats[:, k * head_count : (k + 1) * head_count]
        tops.append(piece(0) + piece(1) + piece(2))
        totals.append(piece(3) + piece(4) + piece(5))
    top = tops[0]
    for other in tops[1:]:
        top = jnp.maximum(top, other)
    scales = [jnp.exp(one - top) for one in tops]
    total = totals[0] * scales[0]
    for one, scale in zip(totals[1:], scales[1:]):
        total = total + one * scale
    lane = lax.broadcasted_iota(jnp.int32, (row_count, 128), 1)
    first_half = lane < HD
    for pair in range(width // 128):
        cols = slice(pair * 128, (pair + 1) * 128)
        pick = lambda per_head: jnp.where(
            first_half, per_head[:, 2 * pair : 2 * pair + 1], per_head[:, 2 * pair + 1 : 2 * pair + 2]
        )
        acc = part_refs[0][:, cols].astype(jnp.float32) * pick(scales[0])
        for ref, scale in zip(part_refs[1:], scales[1:]):
            acc = acc + ref[:, cols].astype(jnp.float32) * pick(scale)
        if finish:
            out_ref[:, cols] = (acc / pick(total)).astype(out_ref.dtype)
        else:
            out_ref[:, cols] = acc
    if not finish:
        stats = jnp.zeros((row_count, 128), jnp.float32)
        for head in range(head_count):
            pieces = split_three(top[:, head : head + 1]) + split_three(total[:, head : head + 1])
            for piece, part in enumerate(pieces):
                stats = jnp.where(lane == piece * head_count + head, part, stats)
        out_ref[:, width : width + 128] = stats


def merge_partials(partials, finish=True):
    row_count, padded = partials[0].shape
    width = padded - 128
    whole = lambda i: (0, 0)
    out_width = width if finish else padded
    out_dtype = jnp.bfloat16 if finish else jnp.float32
    return pl.pallas_call(
        functools.partial(merge_kernel, finish),
        grid=(1,),
        in_specs=[pl.BlockSpec(x.shape, whole) for x in partials],
        out_specs=pl.BlockSpec((row_count, out_width), whole),
        out_shape=jax.ShapeDtypeStruct((row_count, out_width), out_dtype),
    )(*partials)


def combine(current, incoming):
    out_a, top_a, total_a = current
    out_b, top_b, total_b = incoming
    new_top = jnp.maximum(top_a, top_b)
    scale_a = jnp.exp(top_a - new_top)
    scale_b = jnp.exp(top_b - new_top)
    return (
        out_a * scale_a[..., None] + out_b * scale_b[..., None],
        new_top,
        total_a * scale_a + total_b * scale_b,
    )


def window_visible(block_number, cache_len, row_count, block_rows):
    positions = block_number * block_rows + jnp.arange(block_rows, dtype=jnp.int32)
    query_pos = cache_len + jnp.arange(row_count, dtype=jnp.int32)
    return (positions[None, :] > query_pos[:, None] - WINDOW) & (positions[None, :] < cache_len)


def finish_heads(merged):
    summed, row_top, row_total = merged
    result = summed / row_total[..., None]
    head_count, row_count, head_size = result.shape
    return (
        jnp.transpose(result, (1, 0, 2))
        .reshape(row_count, head_count * head_size)
        .astype(jnp.bfloat16)
    )


def head_whole(projected):
    part = projected.astype(jnp.bfloat16)
    other = lax.ppermute(part, "head", [(0, 1), (1, 0)])
    return part.astype(jnp.float32) + other.astype(jnp.float32)


def full_norm(pre_norm, gain_vec, bias_vec):
    row_mean = jnp.mean(pre_norm, axis=-1, keepdims=True)
    centered = pre_norm - row_mean
    row_var = jnp.mean(centered * centered, axis=-1, keepdims=True)
    return centered * lax.rsqrt(row_var + norm_eps) * gain_vec + bias_vec


def project_back(rows_in, weight_t):
    return lax.dot_general(
        rows_in, weight_t, (((1,), (1,)), ((), ())), preferred_element_type=jnp.float32
    )


def per_device(
    queries,
    new_keys,
    new_values,
    sink_keys,
    sink_values,
    pool_keys,
    pool_values,
    block_ids,
    cache_lengths,
    cross_keys,
    cross_values,
    enc_lengths,
    hidden,
    w_out_t,
    gain_self,
    bias_self,
    w_cross_q,
    w_cross_out_t,
    gain_cross,
    bias_cross,
):
    device = lax.axis_index("blk")
    blk_count = lax.axis_size("blk")
    span_rows = queries.shape[0]
    slot_count = pool_keys.shape[1]
    block_rows = pool_keys.shape[2]
    sink_count = sink_keys.shape[1]
    own_length = lax.dynamic_index_in_dim(cache_lengths, device, keepdims=False)
    pad_rows = (-(sink_count + span_rows)) % 16
    pad_block = jnp.zeros((pad_rows, new_keys.shape[1]), new_keys.dtype)
    local_keys = jnp.concatenate([sink_keys[0], new_keys, pad_block], axis=0)
    local_values = jnp.concatenate([sink_values[0], new_values, pad_block], axis=0)
    local_bounds = jnp.array([sink_count, -FAR, sink_count + 1, FAR], jnp.int32)
    local_part = attention_partial(local_bounds, queries, local_keys, local_values, jnp.float32)
    slot_range = jnp.arange(slot_count, dtype=jnp.int32)
    asker_lengths = cache_lengths[(device - slot_range - 1) % blk_count]
    block_starts = lax.dynamic_index_in_dim(block_ids, device, keepdims=False) * block_rows
    bound_table = jnp.stack(
        [
            jnp.zeros_like(block_starts),
            asker_lengths - WINDOW - block_starts,
            jnp.full_like(block_starts, FAR),
            asker_lengths - block_starts,
        ],
        axis=1,
    ).reshape(-1)
    returned = {}
    for slot_step in range(1, slot_count + 1):
        travelling = passed_along(queries, "blk", slot_step)
        remote_part = attention_partial(
            bound_table, travelling, pool_keys[0], pool_values[0], jnp.bfloat16, slot_step - 1,
            after=local_part if slot_step == 1 else None,
        )
        returned[slot_step] = passed_along(remote_part, "blk", -slot_step)
    early = [step for step in EARLY_SLOTS if step <= slot_count]
    late = [step for step in range(1, slot_count + 1) if step not in early]
    partials = [local_part] + [returned[step] for step in early]
    if early:
        partials = [merge_partials(partials, finish=False)]
    attended = merge_partials(partials + [returned[step] for step in late])
    self_proj = project_back(attended, w_out_t)
    head_index = lax.axis_index("head")
    head_width = hidden.shape[1]
    col_start = head_index * head_width
    own_cols = lax.dynamic_slice_in_dim(self_proj, col_start, head_width, 1) + hidden.astype(
        jnp.float32
    )
    with_residual = lax.dynamic_update_slice_in_dim(self_proj, own_cols, col_start, 1)
    pre_full = head_whole(with_residual)
    normed_full = full_norm(pre_full, gain_self, bias_self).astype(jnp.bfloat16)
    cross_query = jnp.dot(normed_full, w_cross_q, preferred_element_type=jnp.float32).astype(
        jnp.bfloat16
    )
    enc_bounds = jnp.stack([0, -FAR, FAR, enc_lengths[0]]).astype(jnp.int32)
    context = merge_partials(
        [attention_partial(enc_bounds, cross_query, cross_keys[0], cross_values[0], jnp.float32)]
    )
    cross_proj = project_back(context, w_cross_out_t)
    own_normed = lax.dynamic_slice_in_dim(normed_full, col_start, head_width, 1).astype(jnp.float32)
    own_cross = lax.dynamic_slice_in_dim(cross_proj, col_start, head_width, 1) + own_normed
    cross_residual = lax.dynamic_update_slice_in_dim(cross_proj, own_cross, col_start, 1)
    second_full = head_whole(cross_residual)
    full_out = full_norm(second_full, gain_cross, bias_cross).astype(jnp.bfloat16)
    layer_out = lax.dynamic_slice_in_dim(full_out, col_start, head_width, 1)
    return layer_out


def solution(mesh):
    placed = (
        P("blk", "head"),
        P("blk", "head"),
        P("blk", "head"),
        P("blk", None, "head"),
        P("blk", None, "head"),
        P("blk", None, None, "head"),
        P("blk", None, None, "head"),
        P(),
        P(),
        P("blk", None, "head"),
        P("blk", None, "head"),
        P("blk"),
        P("blk", "head"),
        P(None, "head"),
        P(),
        P(),
        P(None, "head"),
        P(None, "head"),
        P(),
        P(),
    )
    return jax.shard_map(
        per_device, mesh=mesh, in_specs=placed, out_specs=P("blk", "head"), check_vma=False
    )
```

```python
import functools

import jax
import jax.numpy as jnp
from jax import lax
from jax.experimental import pallas as pl
from jax.experimental.pallas import tpu as pltpu
from jax.sharding import PartitionSpec as P

HD = 64
WINDOW = 4096


masked_score = -1e30
top_floor = -1e20
FAR = 1 << 30
EARLY_SLOTS = (1, 6, 7, 8)
norm_eps = 1e-05


def passed_along(block, axis, distance):
    devices = range(lax.axis_size(axis))
    route = [((i - distance) % len(devices), i) for i in devices]
    return lax.ppermute(block, axis, route)


def partial_block(query_rows, key_rows, value_rows, visible):
    row_count = query_rows.shape[0]
    key_count = key_rows.shape[0]
    head_count = query_rows.shape[1] // HD
    query_heads = query_rows.reshape(row_count, head_count, HD)
    key_heads = key_rows.reshape(key_count, head_count, HD)
    value_heads = value_rows.reshape(key_count, head_count, HD)
    scores = jnp.einsum(
        "qhd,khd->hqk", query_heads, key_heads, preferred_element_type=jnp.float32
    ) * HD ** (-0.5)
    scores = scores + jnp.where(visible, 0.0, masked_score)[None]
    row_top = jnp.maximum(jnp.max(scores, axis=-1), top_floor)
    weights = jnp.exp(scores - row_top[..., None])
    row_total = jnp.sum(weights, axis=-1)
    summed = jnp.einsum(
        "hqk,khd->hqd",
        weights.astype(jnp.bfloat16),
        value_heads,
        preferred_element_type=jnp.float32,
    )
    return (summed, row_top, row_total)


def split_three(values):
    high = values.astype(jnp.bfloat16).astype(jnp.float32)
    rest = values - high
    middle = rest.astype(jnp.bfloat16).astype(jnp.float32)
    low = (rest - middle).astype(jnp.bfloat16).astype(jnp.float32)
    return (high, middle, low)


def window_kernel(offset, finish, bounds_ref, q_ref, k_ref, v_ref, *rest):
    out_ref = rest[-1]
    row_count, width = q_ref.shape
    key_count = k_ref.shape[0]
    head_count = width // HD
    always = bounds_ref[offset]
    low = bounds_ref[offset + 1]
    upper = bounds_ref[offset + 2]
    high = bounds_ref[offset + 3]
    row = lax.broadcasted_iota(jnp.int32, (row_count, key_count), 0)
    col = lax.broadcasted_iota(jnp.int32, (row_count, key_count), 1)
    rel = col - row
    visible = (col < always) | ((rel > low) & (rel < upper) & (col < high))
    bias = jnp.where(visible, 0.0, masked_score)
    lane = lax.broadcasted_iota(jnp.int32, (row_count, 128), 1)
    first_half = lane < HD
    stats = jnp.zeros((row_count, 128), jnp.float32)
    for pair in range(width // 128):
        cols = slice(pair * 128, (pair + 1) * 128)
        q_pair = q_ref[:, cols]
        k_pair = k_ref[:, cols]
        v_pair = v_ref[:, cols]
        out_tile = jnp.zeros((row_count, 128), jnp.float32)
        for half in range(2):
            head = 2 * pair + half
            mine = first_half if half == 0 else jnp.logical_not(first_half)
            q_head = jnp.where(mine, q_pair, jnp.zeros_like(q_pair))
            scores = lax.dot_general(
                q_head, k_pair, (((1,), (1,)), ((), ())), preferred_element_type=jnp.float32
            ) * HD ** (-0.5) + bias
            top = jnp.maximum(jnp.max(scores, axis=1, keepdims=True), top_floor)
            weights = jnp.exp(scores - top)
            total = jnp.sum(weights, axis=1, keepdims=True)
            summed = jnp.dot(
                weights.astype(jnp.bfloat16), v_pair, preferred_element_type=jnp.float32
            )
            if finish:
                summed = summed / total
            out_tile = jnp.where(mine, summed, out_tile)
            for piece, part in enumerate(split_three(top) + split_three(total)):
                stats = jnp.where(lane == piece * head_count + head, part, stats)
        out_ref[:, cols] = out_tile.astype(out_ref.dtype)
    if not finish:
        out_ref[:, width : width + 128] = stats.astype(out_ref.dtype)


def attention_partial(
    bounds, query_rows, key_rows, value_rows, out_dtype, slot=None, after=None, finish=False
):
    row_count, width = query_rows.shape
    key_count = key_rows.shape[-2]
    whole = lambda i: (0, 0)
    if slot is None:
        key_spec = pl.BlockSpec((key_count, width), whole)
        offset = 0
    else:
        offset = 4 * slot
        key_spec = pl.BlockSpec((None, key_count, width), lambda i: (slot, 0, 0))
    operands = [bounds, query_rows, key_rows, value_rows]
    out_width = width if finish else width + 128
    in_specs = [
        pl.BlockSpec(memory_space=pltpu.SMEM),
        pl.BlockSpec((row_count, width), whole),
        key_spec,
        key_spec,
    ]
    if after is not None:
        operands.append(after)
        in_specs.append(pl.BlockSpec(memory_space=pl.ANY))
    return pl.pallas_call(
        functools.partial(window_kernel, offset, finish),
        grid=(1,),
        in_specs=in_specs,
        out_specs=pl.BlockSpec((row_count, out_width), whole),
        out_shape=jax.ShapeDtypeStruct((row_count, out_width), out_dtype),
    )(*operands)


def merge_kernel(finish, *refs):
    part_refs = refs[:-1]
    out_ref = refs[-1]
    row_count = out_ref.shape[0]
    width = part_refs[0].shape[1] - 128
    head_count = width // HD
    tops = []
    totals = []
    for ref in part_refs:
        stats = ref[:, width : width + 128].astype(jnp.float32)
        piece = lambda k: stats[:, k * head_count : (k + 1) * head_count]
        tops.append(piece(0) + piece(1) + piece(2))
        totals.append(piece(3) + piece(4) + piece(5))
    top = tops[0]
    for other in tops[1:]:
        top = jnp.maximum(top, other)
    scales = [jnp.exp(one - top) for one in tops]
    total = totals[0] * scales[0]
    for one, scale in zip(totals[1:], scales[1:]):
        total = total + one * scale
    lane = lax.broadcasted_iota(jnp.int32, (row_count, 128), 1)
    first_half = lane < HD
    for pair in range(width // 128):
        cols = slice(pair * 128, (pair + 1) * 128)
        pick = lambda per_head: jnp.where(
            first_half, per_head[:, 2 * pair : 2 * pair + 1], per_head[:, 2 * pair + 1 : 2 * pair + 2]
        )
        acc = part_refs[0][:, cols].astype(jnp.float32) * pick(scales[0])
        for ref, scale in zip(part_refs[1:], scales[1:]):
            acc = acc + ref[:, cols].astype(jnp.float32) * pick(scale)
        if finish:
            out_ref[:, cols] = (acc / pick(total)).astype(out_ref.dtype)
        else:
            out_ref[:, cols] = acc
    if not finish:
        stats = jnp.zeros((row_count, 128), jnp.float32)
        for head in range(head_count):
            pieces = split_three(top[:, head : head + 1]) + split_three(total[:, head : head + 1])
            for piece, part in enumerate(pieces):
                stats = jnp.where(lane == piece * head_count + head, part, stats)
        out_ref[:, width : width + 128] = stats


def merge_partials(partials, finish=True):
    row_count, padded = partials[0].shape
    width = padded - 128
    whole = lambda i: (0, 0)
    out_width = width if finish else padded
    out_dtype = jnp.bfloat16 if finish else jnp.float32
    return pl.pallas_call(
        functools.partial(merge_kernel, finish),
        grid=(1,),
        in_specs=[pl.BlockSpec(x.shape, whole) for x in partials],
        out_specs=pl.BlockSpec((row_count, out_width), whole),
        out_shape=jax.ShapeDtypeStruct((row_count, out_width), out_dtype),
    )(*partials)


def combine(current, incoming):
    out_a, top_a, total_a = current
    out_b, top_b, total_b = incoming
    new_top = jnp.maximum(top_a, top_b)
    scale_a = jnp.exp(top_a - new_top)
    scale_b = jnp.exp(top_b - new_top)
    return (
        out_a * scale_a[..., None] + out_b * scale_b[..., None],
        new_top,
        total_a * scale_a + total_b * scale_b,
    )


def window_visible(block_number, cache_len, row_count, block_rows):
    positions = block_number * block_rows + jnp.arange(block_rows, dtype=jnp.int32)
    query_pos = cache_len + jnp.arange(row_count, dtype=jnp.int32)
    return (positions[None, :] > query_pos[:, None] - WINDOW) & (positions[None, :] < cache_len)


def finish_heads(merged):
    summed, row_top, row_total = merged
    result = summed / row_total[..., None]
    head_count, row_count, head_size = result.shape
    return (
        jnp.transpose(result, (1, 0, 2))
        .reshape(row_count, head_count * head_size)
        .astype(jnp.bfloat16)
    )


def head_whole(projected):
    part = projected.astype(jnp.bfloat16)
    other = lax.ppermute(part, "head", [(0, 1), (1, 0)])
    return part.astype(jnp.float32) + other.astype(jnp.float32)


def full_norm(pre_norm, gain_vec, bias_vec):
    row_mean = jnp.mean(pre_norm, axis=-1, keepdims=True)
    centered = pre_norm - row_mean
    row_var = jnp.mean(centered * centered, axis=-1, keepdims=True)
    return centered * lax.rsqrt(row_var + norm_eps) * gain_vec + bias_vec


def project_back(rows_in, weight_t):
    return lax.dot_general(
        rows_in, weight_t, (((1,), (1,)), ((), ())), preferred_element_type=jnp.float32
    )


def per_device(
    queries,
    new_keys,
    new_values,
    sink_keys,
    sink_values,
    pool_keys,
    pool_values,
    block_ids,
    cache_lengths,
    cross_keys,
    cross_values,
    enc_lengths,
    hidden,
    w_out_t,
    gain_self,
    bias_self,
    w_cross_q,
    w_cross_out_t,
    gain_cross,
    bias_cross,
):
    device = lax.axis_index("blk")
    blk_count = lax.axis_size("blk")
    span_rows = queries.shape[0]
    slot_count = pool_keys.shape[1]
    block_rows = pool_keys.shape[2]
    sink_count = sink_keys.shape[1]
    own_length = lax.dynamic_index_in_dim(cache_lengths, device, keepdims=False)
    pad_rows = (-(sink_count + span_rows)) % 16
    pad_block = jnp.zeros((pad_rows, new_keys.shape[1]), new_keys.dtype)
    local_keys = jnp.concatenate([sink_keys[0], new_keys, pad_block], axis=0)
    local_values = jnp.concatenate([sink_values[0], new_values, pad_block], axis=0)
    local_bounds = jnp.array([sink_count, -FAR, sink_count + 1, FAR], jnp.int32)
    local_part = attention_partial(local_bounds, queries, local_keys, local_values, jnp.float32)
    slot_range = jnp.arange(slot_count, dtype=jnp.int32)
    asker_lengths = cache_lengths[(device - slot_range - 1) % blk_count]
    block_starts = lax.dynamic_index_in_dim(block_ids, device, keepdims=False) * block_rows
    bound_table = jnp.stack(
        [
            jnp.zeros_like(block_starts),
            asker_lengths - WINDOW - block_starts,
            jnp.full_like(block_starts, FAR),
            asker_lengths - block_starts,
        ],
        axis=1,
    ).reshape(-1)
    returned = {}
    for slot_step in range(1, slot_count + 1):
        travelling = passed_along(queries, "blk", slot_step)
        remote_part = attention_partial(
            bound_table, travelling, pool_keys[0], pool_values[0], jnp.bfloat16, slot_step - 1,
            after=local_part if slot_step == 1 else None,
        )
        returned[slot_step] = passed_along(remote_part, "blk", -slot_step)
    early = [step for step in EARLY_SLOTS if step <= slot_count]
    late = [step for step in range(1, slot_count + 1) if step not in early]
    partials = [local_part] + [returned[step] for step in early]
    if early:
        partials = [merge_partials(partials, finish=False)]
    attended = merge_partials(partials + [returned[step] for step in late])
    self_proj = project_back(attended, w_out_t)
    head_index = lax.axis_index("head")
    head_width = hidden.shape[1]
    col_start = head_index * head_width
    own_cols = lax.dynamic_slice_in_dim(self_proj, col_start, head_width, 1) + hidden.astype(
        jnp.float32
    )
    with_residual = lax.dynamic_update_slice_in_dim(self_proj, own_cols, col_start, 1)
    pre_full = head_whole(with_residual)
    normed_full = full_norm(pre_full, gain_self, bias_self).astype(jnp.bfloat16)
    cross_query = jnp.dot(normed_full, w_cross_q, preferred_element_type=jnp.float32).astype(
        jnp.bfloat16
    )
    enc_bounds = jnp.stack([0, -FAR, FAR, enc_lengths[0]]).astype(jnp.int32)
    context = attention_partial(
        enc_bounds, cross_query, cross_keys[0], cross_values[0], jnp.bfloat16, finish=True
    )
    cross_proj = project_back(context, w_cross_out_t)
    own_normed = lax.dynamic_slice_in_dim(normed_full, col_start, head_width, 1).astype(jnp.float32)
    own_cross = lax.dynamic_slice_in_dim(cross_proj, col_start, head_width, 1) + own_normed
    cross_residual = lax.dynamic_update_slice_in_dim(cross_proj, own_cross, col_start, 1)
    second_full = head_whole(cross_residual)
    full_out = full_norm(second_full, gain_cross, bias_cross).astype(jnp.bfloat16)
    layer_out = lax.dynamic_slice_in_dim(full_out, col_start, head_width, 1)
    return layer_out


def solution(mesh):
    placed = (
        P("blk", "head"),
        P("blk", "head"),
        P("blk", "head"),
        P("blk", None, "head"),
        P("blk", None, "head"),
        P("blk", None, None, "head"),
        P("blk", None, None, "head"),
        P(),
        P(),
        P("blk", None, "head"),
        P("blk", None, "head"),
        P("blk"),
        P("blk", "head"),
        P(None, "head"),
        P(),
        P(),
        P(None, "head"),
        P(None, "head"),
        P(),
        P(),
    )
    return jax.shard_map(
        per_device, mesh=mesh, in_specs=placed, out_specs=P("blk", "head"), check_vma=False
    )
```

```python
import functools

import jax
import jax.numpy as jnp
from jax import lax
from jax.experimental import pallas as pl
from jax.experimental.pallas import tpu as pltpu
from jax.sharding import PartitionSpec as P

HD = 64
WINDOW = 4096


masked_score = -1e30
top_floor = -1e20
FAR = 1 << 30
MERGE_STAGES = ((1, 6, 7, 8), (9, 2, 3))
norm_eps = 1e-05


def passed_along(block, axis, distance):
    devices = range(lax.axis_size(axis))
    route = [((i - distance) % len(devices), i) for i in devices]
    return lax.ppermute(block, axis, route)


def partial_block(query_rows, key_rows, value_rows, visible):
    row_count = query_rows.shape[0]
    key_count = key_rows.shape[0]
    head_count = query_rows.shape[1] // HD
    query_heads = query_rows.reshape(row_count, head_count, HD)
    key_heads = key_rows.reshape(key_count, head_count, HD)
    value_heads = value_rows.reshape(key_count, head_count, HD)
    scores = jnp.einsum(
        "qhd,khd->hqk", query_heads, key_heads, preferred_element_type=jnp.float32
    ) * HD ** (-0.5)
    scores = scores + jnp.where(visible, 0.0, masked_score)[None]
    row_top = jnp.maximum(jnp.max(scores, axis=-1), top_floor)
    weights = jnp.exp(scores - row_top[..., None])
    row_total = jnp.sum(weights, axis=-1)
    summed = jnp.einsum(
        "hqk,khd->hqd",
        weights.astype(jnp.bfloat16),
        value_heads,
        preferred_element_type=jnp.float32,
    )
    return (summed, row_top, row_total)


def split_three(values):
    high = values.astype(jnp.bfloat16).astype(jnp.float32)
    rest = values - high
    middle = rest.astype(jnp.bfloat16).astype(jnp.float32)
    low = (rest - middle).astype(jnp.bfloat16).astype(jnp.float32)
    return (high, middle, low)


def window_kernel(offset, finish, bounds_ref, q_ref, k_ref, v_ref, *rest):
    out_ref = rest[-1]
    row_count, width = q_ref.shape
    key_count = k_ref.shape[0]
    head_count = width // HD
    always = bounds_ref[offset]
    low = bounds_ref[offset + 1]
    upper = bounds_ref[offset + 2]
    high = bounds_ref[offset + 3]
    row = lax.broadcasted_iota(jnp.int32, (row_count, key_count), 0)
    col = lax.broadcasted_iota(jnp.int32, (row_count, key_count), 1)
    rel = col - row
    visible = (col < always) | ((rel > low) & (rel < upper) & (col < high))
    bias = jnp.where(visible, 0.0, masked_score)
    lane = lax.broadcasted_iota(jnp.int32, (row_count, 128), 1)
    first_half = lane < HD
    stats = jnp.zeros((row_count, 128), jnp.float32)
    for pair in range(width // 128):
        cols = slice(pair * 128, (pair + 1) * 128)
        q_pair = q_ref[:, cols]
        k_pair = k_ref[:, cols]
        v_pair = v_ref[:, cols]
        out_tile = jnp.zeros((row_count, 128), jnp.float32)
        for half in range(2):
            head = 2 * pair + half
            mine = first_half if half == 0 else jnp.logical_not(first_half)
            q_head = jnp.where(mine, q_pair, jnp.zeros_like(q_pair))
            scores = lax.dot_general(
                q_head, k_pair, (((1,), (1,)), ((), ())), preferred_element_type=jnp.float32
            ) * HD ** (-0.5) + bias
            top = jnp.maximum(jnp.max(scores, axis=1, keepdims=True), top_floor)
            weights = jnp.exp(scores - top)
            total = jnp.sum(weights, axis=1, keepdims=True)
            summed = jnp.dot(
                weights.astype(jnp.bfloat16), v_pair, preferred_element_type=jnp.float32
            )
            if finish:
                summed = summed / total
            out_tile = jnp.where(mine, summed, out_tile)
            for piece, part in enumerate(split_three(top) + split_three(total)):
                stats = jnp.where(lane == piece * head_count + head, part, stats)
        out_ref[:, cols] = out_tile.astype(out_ref.dtype)
    if not finish:
        out_ref[:, width : width + 128] = stats.astype(out_ref.dtype)


def attention_partial(
    bounds, query_rows, key_rows, value_rows, out_dtype, slot=None, after=None, finish=False
):
    row_count, width = query_rows.shape
    key_count = key_rows.shape[-2]
    whole = lambda i: (0, 0)
    if slot is None:
        key_spec = pl.BlockSpec((key_count, width), whole)
        offset = 0
    else:
        offset = 4 * slot
        key_spec = pl.BlockSpec((None, key_count, width), lambda i: (slot, 0, 0))
    operands = [bounds, query_rows, key_rows, value_rows]
    out_width = width if finish else width + 128
    in_specs = [
        pl.BlockSpec(memory_space=pltpu.SMEM),
        pl.BlockSpec((row_count, width), whole),
        key_spec,
        key_spec,
    ]
    if after is not None:
        operands.append(after)
        in_specs.append(pl.BlockSpec(memory_space=pl.ANY))
    return pl.pallas_call(
        functools.partial(window_kernel, offset, finish),
        grid=(1,),
        in_specs=in_specs,
        out_specs=pl.BlockSpec((row_count, out_width), whole),
        out_shape=jax.ShapeDtypeStruct((row_count, out_width), out_dtype),
    )(*operands)


def merge_kernel(finish, *refs):
    part_refs = refs[:-1]
    out_ref = refs[-1]
    row_count = out_ref.shape[0]
    width = part_refs[0].shape[1] - 128
    head_count = width // HD
    tops = []
    totals = []
    for ref in part_refs:
        stats = ref[:, width : width + 128].astype(jnp.float32)
        piece = lambda k: stats[:, k * head_count : (k + 1) * head_count]
        tops.append(piece(0) + piece(1) + piece(2))
        totals.append(piece(3) + piece(4) + piece(5))
    top = tops[0]
    for other in tops[1:]:
        top = jnp.maximum(top, other)
    scales = [jnp.exp(one - top) for one in tops]
    total = totals[0] * scales[0]
    for one, scale in zip(totals[1:], scales[1:]):
        total = total + one * scale
    lane = lax.broadcasted_iota(jnp.int32, (row_count, 128), 1)
    first_half = lane < HD
    for pair in range(width // 128):
        cols = slice(pair * 128, (pair + 1) * 128)
        pick = lambda per_head: jnp.where(
            first_half, per_head[:, 2 * pair : 2 * pair + 1], per_head[:, 2 * pair + 1 : 2 * pair + 2]
        )
        acc = part_refs[0][:, cols].astype(jnp.float32) * pick(scales[0])
        for ref, scale in zip(part_refs[1:], scales[1:]):
            acc = acc + ref[:, cols].astype(jnp.float32) * pick(scale)
        if finish:
            out_ref[:, cols] = (acc / pick(total)).astype(out_ref.dtype)
        else:
            out_ref[:, cols] = acc
    if not finish:
        stats = jnp.zeros((row_count, 128), jnp.float32)
        for head in range(head_count):
            pieces = split_three(top[:, head : head + 1]) + split_three(total[:, head : head + 1])
            for piece, part in enumerate(pieces):
                stats = jnp.where(lane == piece * head_count + head, part, stats)
        out_ref[:, width : width + 128] = stats


def merge_partials(partials, finish=True):
    row_count, padded = partials[0].shape
    width = padded - 128
    whole = lambda i: (0, 0)
    out_width = width if finish else padded
    out_dtype = jnp.bfloat16 if finish else jnp.float32
    return pl.pallas_call(
        functools.partial(merge_kernel, finish),
        grid=(1,),
        in_specs=[pl.BlockSpec(x.shape, whole) for x in partials],
        out_specs=pl.BlockSpec((row_count, out_width), whole),
        out_shape=jax.ShapeDtypeStruct((row_count, out_width), out_dtype),
    )(*partials)


def combine(current, incoming):
    out_a, top_a, total_a = current
    out_b, top_b, total_b = incoming
    new_top = jnp.maximum(top_a, top_b)
    scale_a = jnp.exp(top_a - new_top)
    scale_b = jnp.exp(top_b - new_top)
    return (
        out_a * scale_a[..., None] + out_b * scale_b[..., None],
        new_top,
        total_a * scale_a + total_b * scale_b,
    )


def window_visible(block_number, cache_len, row_count, block_rows):
    positions = block_number * block_rows + jnp.arange(block_rows, dtype=jnp.int32)
    query_pos = cache_len + jnp.arange(row_count, dtype=jnp.int32)
    return (positions[None, :] > query_pos[:, None] - WINDOW) & (positions[None, :] < cache_len)


def finish_heads(merged):
    summed, row_top, row_total = merged
    result = summed / row_total[..., None]
    head_count, row_count, head_size = result.shape
    return (
        jnp.transpose(result, (1, 0, 2))
        .reshape(row_count, head_count * head_size)
        .astype(jnp.bfloat16)
    )


def head_whole(projected):
    part = projected.astype(jnp.bfloat16)
    other = lax.ppermute(part, "head", [(0, 1), (1, 0)])
    return part.astype(jnp.float32) + other.astype(jnp.float32)


def full_norm(pre_norm, gain_vec, bias_vec):
    row_mean = jnp.mean(pre_norm, axis=-1, keepdims=True)
    centered = pre_norm - row_mean
    row_var = jnp.mean(centered * centered, axis=-1, keepdims=True)
    return centered * lax.rsqrt(row_var + norm_eps) * gain_vec + bias_vec


def project_back(rows_in, weight_t):
    return lax.dot_general(
        rows_in, weight_t, (((1,), (1,)), ((), ())), preferred_element_type=jnp.float32
    )


def per_device(
    queries,
    new_keys,
    new_values,
    sink_keys,
    sink_values,
    pool_keys,
    pool_values,
    block_ids,
    cache_lengths,
    cross_keys,
    cross_values,
    enc_lengths,
    hidden,
    w_out_t,
    gain_self,
    bias_self,
    w_cross_q,
    w_cross_out_t,
    gain_cross,
    bias_cross,
):
    device = lax.axis_index("blk")
    blk_count = lax.axis_size("blk")
    span_rows = queries.shape[0]
    slot_count = pool_keys.shape[1]
    block_rows = pool_keys.shape[2]
    sink_count = sink_keys.shape[1]
    own_length = lax.dynamic_index_in_dim(cache_lengths, device, keepdims=False)
    pad_rows = (-(sink_count + span_rows)) % 16
    pad_block = jnp.zeros((pad_rows, new_keys.shape[1]), new_keys.dtype)
    local_keys = jnp.concatenate([sink_keys[0], new_keys, pad_block], axis=0)
    local_values = jnp.concatenate([sink_values[0], new_values, pad_block], axis=0)
    local_bounds = jnp.array([sink_count, -FAR, sink_count + 1, FAR], jnp.int32)
    local_part = attention_partial(local_bounds, queries, local_keys, local_values, jnp.float32)
    slot_range = jnp.arange(slot_count, dtype=jnp.int32)
    asker_lengths = cache_lengths[(device - slot_range - 1) % blk_count]
    block_starts = lax.dynamic_index_in_dim(block_ids, device, keepdims=False) * block_rows
    bound_table = jnp.stack(
        [
            jnp.zeros_like(block_starts),
            asker_lengths - WINDOW - block_starts,
            jnp.full_like(block_starts, FAR),
            asker_lengths - block_starts,
        ],
        axis=1,
    ).reshape(-1)
    returned = {}
    for slot_step in range(1, slot_count + 1):
        travelling = passed_along(queries, "blk", slot_step)
        remote_part = attention_partial(
            bound_table, travelling, pool_keys[0], pool_values[0], jnp.bfloat16, slot_step - 1,
            after=local_part if slot_step == 1 else None,
        )
        returned[slot_step] = passed_along(remote_part, "blk", -slot_step)
    partials = [local_part]
    merged_steps = set()
    for stage in MERGE_STAGES:
        steps = [step for step in stage if step <= slot_count and step not in merged_steps]
        if steps:
            partials = [merge_partials(partials + [returned[step] for step in steps], finish=False)]
            merged_steps.update(steps)
    late = [step for step in range(1, slot_count + 1) if step not in merged_steps]
    attended = merge_partials(partials + [returned[step] for step in late])
    self_proj = project_back(attended, w_out_t)
    head_index = lax.axis_index("head")
    head_width = hidden.shape[1]
    col_start = head_index * head_width
    own_cols = lax.dynamic_slice_in_dim(self_proj, col_start, head_width, 1) + hidden.astype(
        jnp.float32
    )
    with_residual = lax.dynamic_update_slice_in_dim(self_proj, own_cols, col_start, 1)
    pre_full = head_whole(with_residual)
    normed_full = full_norm(pre_full, gain_self, bias_self).astype(jnp.bfloat16)
    cross_query = jnp.dot(normed_full, w_cross_q, preferred_element_type=jnp.float32).astype(
        jnp.bfloat16
    )
    enc_bounds = jnp.stack([0, -FAR, FAR, enc_lengths[0]]).astype(jnp.int32)
    context = attention_partial(
        enc_bounds, cross_query, cross_keys[0], cross_values[0], jnp.bfloat16, finish=True
    )
    cross_proj = project_back(context, w_cross_out_t)
    own_normed = lax.dynamic_slice_in_dim(normed_full, col_start, head_width, 1).astype(jnp.float32)
    own_cross = lax.dynamic_slice_in_dim(cross_proj, col_start, head_width, 1) + own_normed
    cross_residual = lax.dynamic_update_slice_in_dim(cross_proj, own_cross, col_start, 1)
    second_full = head_whole(cross_residual)
    full_out = full_norm(second_full, gain_cross, bias_cross).astype(jnp.bfloat16)
    layer_out = lax.dynamic_slice_in_dim(full_out, col_start, head_width, 1)
    return layer_out


def solution(mesh):
    placed = (
        P("blk", "head"),
        P("blk", "head"),
        P("blk", "head"),
        P("blk", None, "head"),
        P("blk", None, "head"),
        P("blk", None, None, "head"),
        P("blk", None, None, "head"),
        P(),
        P(),
        P("blk", None, "head"),
        P("blk", None, "head"),
        P("blk"),
        P("blk", "head"),
        P(None, "head"),
        P(),
        P(),
        P(None, "head"),
        P(None, "head"),
        P(),
        P(),
    )
    return jax.shard_map(
        per_device, mesh=mesh, in_specs=placed, out_specs=P("blk", "head"), check_vma=False
    )
```
